128 devices in a mesh: lat: 16 (over z_lo, x, core), freq: 8 (over z_hi, y).
Axes of the slice: x: 4, y: 4, z: 4 (z_hi: 2, z_lo: 2; z = z_hi * 2 + z_lo), core: 2. Of those that a mesh axis runs over, the one named last changes fastest.
Arguments:
- gravity: float32 [256, 21600], P('lat', 'freq'), may hold values from -6 to 6
- coef: bfloat16 [2176, 2, 2176], P(('lat', 'freq')), may hold values from -0.125 to 0.125
- legendre: bfloat16 [2176, 2176, 256], P(('lat', 'freq')), may hold values from -6 to 6
- order_table: int32 [2176], replicated, may hold values from 0 to 2175, as said below
- band_rows: int32 [256], P('lat'), may hold values from 0 to 2399, as said below
- kernel: bfloat16 [511, 10800], P(None, 'freq'), may hold values from -0.375 to 0.375
Outputs:
- geoid: float32 [256, 21600], P('lat', 'freq')
The draws below stay inside these ranges and needn't reach their ends.
Inputs may be any that keep to these rules, and one draw needn't show every extreme that they name: `order_table`: A permutation of the orders 0 to 2175; the slot s lies in the block of slots s // 17, and its order m has m % 8 == (s // 17) % 8. `band_rows`: strictly increasing; the first row is parallel 0 and the last is parallel 2400 - 1.
All inputs are finite; a program needn't handle non-finite values.
Results may differ from the reference program's by a relative error of at most 0.0032.
Values may be sent and summed in bfloat16 or wider, within the bound.
No kernel may reach another device: no remote copies, remote signals or barrier semaphores. Data moves between devices by JAX's collectives and lax.ppermute only.
A program may use at most 128 MiB of HBM per device.

```python
import jax
import jax.numpy as jnp
from jax import lax

L = 21600
K = 10800
NORD = 2176
NDEG = 2176
R = 16
PARALLELS = 2400
NBLK = 16
NBAND = 8
RT = 256
OPD = 17
KB = 1350


def group_permutation(subkey):
    return jax.random.permutation(subkey, NORD // NBAND)


def draw_order_table(key, part):
    keys_all = jax.random.split(jax.random.fold_in(key, 11), NBAND)
    perms = jax.vmap(group_permutation)(keys_all)
    slots = jnp.arange(NORD, dtype=jnp.int32)
    block = slots // OPD
    lat_index = block // NBAND
    band = block % NBAND
    within = slots % OPD
    return (perms[band, lat_index * OPD + within] * NBAND + band).astype(jnp.int32)


def draw_band_rows(key, part):
    inner = jax.random.permutation(jax.random.fold_in(key, 17), PARALLELS - 2)[:RT - 2] + 1
    chosen = jnp.sort(inner).astype(jnp.int32)
    first = jnp.zeros((1,), jnp.int32)
    last = jnp.full((1,), PARALLELS - 1, jnp.int32)
    return jnp.concatenate([first, chosen, last])


def steps_of(key, shape, cuts, least, largest):
    level, own = 1.0, jax.random.fold_in(key, 6)
    for dim, blocks in cuts:
        heights = jnp.exp(jax.random.uniform(jax.random.fold_in(own, dim), (blocks,), jnp.float32, least / len(cuts), largest / len(cuts)))
        level = level * jnp.repeat(heights, shape[dim] // blocks).reshape([-1 if axis == dim else 1 for axis in range(len(shape))])
    return level


def scatter_about(key, shape, scale, most, pieces=(), held_as=jnp.bfloat16):
    array = scale * jax.random.normal(key, shape, jnp.float32)
    if pieces:
        array = array * steps_of(key, shape, pieces, -0.22, 0.18)
    return jnp.clip(array, -most, most).astype(held_as)


def setup_inputs(seed: int = 0) -> dict:
    arg_keys = jax.random.split(jax.random.key(seed), 7)
    return {
        "gravity": scatter_about(arg_keys[0], (RT, L), 1.0, 6.0, ((0, 16), (1, 8)), jnp.float32),
        "coef": scatter_about(arg_keys[1], (NORD, 2, NDEG), NDEG ** -0.5, 0.125, ((0, 128),)),
        "legendre": scatter_about(arg_keys[2], (NORD, NDEG, RT), 1.0, 6.0, ((0, 128),)),
        "order_table": draw_order_table(jax.random.fold_in(arg_keys[6], 71), 0),
        "band_rows": draw_band_rows(jax.random.fold_in(arg_keys[6], 71), 0),
        "kernel": scatter_about(arg_keys[5], (2 * RT - 1, K), RT ** -0.5, 0.375, ((1, 8),)),
    }


def reference(gravity, coef, legendre, order_table, band_rows, kernel):
    scale = (2.0 / L) ** 0.5
    spectrum = jnp.fft.fft(gravity, axis=1)[:, :K] * scale
    synth = jnp.einsum('ocn,onq->ocq', coef.astype(jnp.float32), legendre.astype(jnp.float32), precision=lax.Precision.HIGHEST)
    synth = synth.astype(jnp.bfloat16).astype(jnp.float32)
    model_re = jnp.zeros((RT, K), jnp.float32).at[:, order_table].set(synth[:, 0, :].T)
    model_im = jnp.zeros((RT, K), jnp.float32).at[:, order_table].set(synth[:, 1, :].T)
    weight = jnp.cos((20.0 + band_rows.astype(jnp.float32) / 60.0) * (jnp.pi / 180.0))
    weighted = jnp.stack([spectrum.real - model_re, spectrum.imag - model_im]) * weight[None, :, None]
    weighted = weighted.astype(jnp.bfloat16).astype(jnp.float32)
    kernel_freq = kernel.astype(jnp.float32).reshape(2 * RT - 1, NBAND, KB).transpose(0, 2, 1).reshape(2 * RT - 1, K)

    def one_block(first):
        targets = first + jnp.arange(R, dtype=jnp.int32)
        position = jnp.arange(RT, dtype=jnp.int32)[None, :] - targets[:, None] + RT - 1
        toeplitz = kernel_freq[position]
        return jnp.einsum('pqk,cqk->cpk', toeplitz, weighted, precision=lax.Precision.HIGHEST)

    blocks_out = lax.map(one_block, jnp.arange(NBLK, dtype=jnp.int32) * R)
    stokes = blocks_out.transpose(1, 0, 2, 3).reshape(2, RT, K)
    padded = jnp.pad(stokes[0] + 1j * stokes[1], ((0, 0), (0, L - K)))
    geoid = jnp.fft.ifft(padded, axis=1).real * (L * scale)
    return geoid.astype(jnp.float32)
```

```python
import jax
import jax.numpy as jnp
import numpy as np
from jax import lax
from jax.sharding import PartitionSpec as P
from jax.experimental import pallas as pl
from jax.experimental.pallas import tpu as pltpu

L = 21600
PA = 144
PB = 150
PH = 75


highest = lax.Precision.HIGHEST


def angle_table(first, second, period):
    phase = first * second % period
    return phase.astype(jnp.float32) * (2.0 * np.pi / period)


def forward_bands(grid, first_start, bands):
    rows = grid.shape[0]
    count_one = grid.shape[1]
    first_index = first_start + jnp.arange(count_one, dtype=jnp.int32)
    freq_one = jnp.arange(PA, dtype=jnp.int32)
    theta_one = angle_table(first_index[:, None], freq_one[None, :], PA)
    section_re = jnp.einsum("rab,ak->rbk", grid, jnp.cos(theta_one), precision=highest)
    section_im = -jnp.einsum("rab,ak->rbk", grid, jnp.sin(theta_one), precision=highest)
    second_index = jnp.arange(PB, dtype=jnp.int32)
    twist = angle_table(second_index[:, None], freq_one[None, :], L)
    twist_cos = jnp.cos(twist)
    twist_sin = jnp.sin(twist)
    turned_re = section_re * twist_cos + section_im * twist_sin
    turned_im = section_im * twist_cos - section_re * twist_sin
    freq_two = jnp.arange(PH, dtype=jnp.int32)
    theta_two = angle_table(second_index[:, None], freq_two[None, :], PB)
    cos_two = jnp.cos(theta_two)
    sin_two = jnp.sin(theta_two)
    spec_re = jnp.einsum("rbk,bm->rkm", turned_re, cos_two, precision=highest) + jnp.einsum(
        "rbk,bm->rkm", turned_im, sin_two, precision=highest
    )
    spec_im = jnp.einsum("rbk,bm->rkm", turned_im, cos_two, precision=highest) - jnp.einsum(
        "rbk,bm->rkm", turned_re, sin_two, precision=highest
    )
    scale = (2.0 / L) ** 0.5
    stacked = jnp.stack([spec_re, spec_im]) * scale
    span = PA // bands
    stacked = stacked.reshape(2, rows, span, bands, PH).transpose(3, 1, 0, 4, 2)
    return stacked.reshape(bands, rows, 2, PH * span)


def inverse_rows(spectra, band_ids, bands):
    count = spectra.shape[0]
    rows = spectra.shape[1]
    span = PA // bands
    parts = spectra.reshape(count, rows, 2, PH, span)
    part_re = parts[:, :, 0]
    part_im = parts[:, :, 1]
    freq_two = jnp.arange(PH, dtype=jnp.int32)
    second_index = jnp.arange(PB, dtype=jnp.int32)
    theta_two = angle_table(freq_two[:, None], second_index[None, :], PB)
    cos_two = jnp.cos(theta_two)
    sin_two = jnp.sin(theta_two)
    middle_re = jnp.einsum("brms,mn->brsn", part_re, cos_two, precision=highest) - jnp.einsum(
        "brms,mn->brsn", part_im, sin_two, precision=highest
    )
    middle_im = jnp.einsum("brms,mn->brsn", part_im, cos_two, precision=highest) + jnp.einsum(
        "brms,mn->brsn", part_re, sin_two, precision=highest
    )
    freq_one = jnp.arange(span, dtype=jnp.int32)[None, :] * bands + band_ids[:, None]
    twist = angle_table(freq_one[:, :, None], second_index[None, None, :], L)
    twist_cos = jnp.cos(twist)[:, None]
    twist_sin = jnp.sin(twist)[:, None]
    turned_re = middle_re * twist_cos - middle_im * twist_sin
    turned_im = middle_re * twist_sin + middle_im * twist_cos
    first_index = jnp.arange(PA, dtype=jnp.int32)
    theta_one = angle_table(freq_one[:, :, None], first_index[None, None, :], PA)
    grid = jnp.einsum(
        "brsn,bsa->ran", turned_re, jnp.cos(theta_one), precision=highest
    ) - jnp.einsum("brsn,bsa->ran", turned_im, jnp.sin(theta_one), precision=highest)
    return grid * (2.0 / L) ** 0.5


LANE = 128


def stokes_body(k_ref, w_ref, o_ref, sh_ref):
    shifts = sh_ref.shape[0]
    span = sh_ref.shape[1]
    steps = w_ref.shape[1] // shifts
    width = o_ref.shape[1]
    for r in range(shifts):
        sh_ref[r] = k_ref[pl.ds(r, span), :]

    def step(a, carry):
        acc_re, acc_im = carry
        base = pl.multiple_of(a * shifts, shifts)
        w_re = w_ref[0, pl.ds(base, shifts), :]
        w_im = w_ref[1, pl.ds(base, shifts), :]
        for r in range(shifts):
            slab = sh_ref[r, pl.ds(base, width), :]
            acc_re = acc_re + slab * w_re[r : r + 1, :]
            acc_im = acc_im + slab * w_im[r : r + 1, :]
        return acc_re, acc_im

    zero = jnp.zeros(o_ref.shape[1:], jnp.float32)
    acc_re, acc_im = lax.fori_loop(0, steps, step, (zero, zero))
    o_ref[0] = acc_re
    o_ref[1] = acc_im


def toeplitz_stokes(kernel, weighted, block_self, rows, blocks):
    total_rows = rows * blocks
    width = kernel.shape[1]
    padded = -(-width // LANE) * LANE
    shifts = 8
    everyone = lax.all_gather(weighted, "lat", axis=0, tiled=True)
    first = (blocks - 1 - block_self) * rows
    used = total_rows + rows - 1
    window = lax.dynamic_slice_in_dim(kernel, first, used, 0).astype(jnp.float32)
    window = jnp.pad(window, ((0, -used % shifts), (0, padded - width)))
    source = jnp.pad(
        everyone.astype(jnp.float32).transpose(1, 0, 2), ((0, 0), (0, 0), (0, padded - width))
    )
    span = total_rows + shifts
    out = pl.pallas_call(
        stokes_body,
        grid=(padded // LANE,),
        in_specs=[
            pl.BlockSpec((window.shape[0], LANE), lambda j: (0, j)),
            pl.BlockSpec((2, total_rows, LANE), lambda j: (0, 0, j)),
        ],
        out_specs=pl.BlockSpec((2, rows, LANE), lambda j: (0, 0, j)),
        out_shape=jax.ShapeDtypeStruct((2, rows, padded), jnp.float32),
        scratch_shapes=[pltpu.VMEM((shifts, span, LANE), jnp.float32)],
    )(window, source)
    return out[:, ::-1, :width].transpose(1, 0, 2)


def per_device(gravity, coef, legendre, order_table, band_rows, kernel):
    bands = lax.axis_size("freq")
    blocks = lax.axis_size("lat")
    band_self = lax.axis_index("freq")
    block_self = lax.axis_index("lat")
    rows = gravity.shape[0]
    span = PA // bands
    local_grid = gravity.reshape(rows, span, PB)
    terms = forward_bands(local_grid, band_self * span, bands)
    observed = lax.psum_scatter(terms, "freq", scatter_dimension=0, tiled=True)[0]
    band_width = observed.shape[2]
    synth = jnp.einsum("ocn,onq->ocq", coef, legendre, preferred_element_type=jnp.float32).astype(
        jnp.bfloat16
    )
    routed = lax.all_to_all(synth, "lat", split_axis=2, concat_axis=0, tiled=True)
    per_slot = coef.shape[0]
    slot_ids = (
        (jnp.arange(blocks, dtype=jnp.int32)[:, None] * bands + band_self) * per_slot
        + jnp.arange(per_slot, dtype=jnp.int32)[None, :]
    ).reshape(-1)
    positions = order_table[slot_ids] // bands
    selector = (positions[:, None] == jnp.arange(band_width, dtype=jnp.int32)[None, :]).astype(
        jnp.bfloat16
    )
    model = jnp.einsum("jcr,jt->rct", routed, selector, preferred_element_type=jnp.float32)
    weight = jnp.cos((20.0 + band_rows.astype(jnp.float32) / 60.0) * (np.pi / 180.0))
    weighted = ((observed - model) * weight[:, None, None]).astype(jnp.bfloat16)
    stokes = toeplitz_stokes(kernel, weighted, block_self, rows, blocks)
    grid_terms = inverse_rows(stokes[None], jnp.reshape(band_self, (1,)), bands)
    geoid = lax.psum_scatter(grid_terms, "freq", scatter_dimension=1, tiled=True)
    return geoid.reshape(rows, span * PB)


def solution(mesh):
    return jax.shard_map(
        per_device,
        mesh=mesh,
        in_specs=(
            P("lat", "freq"),
            P(("lat", "freq"), None, None),
            P(("lat", "freq"), None, None),
            P(),
            P("lat"),
            P(None, "freq"),
        ),
        out_specs=P("lat", "freq"),
        check_vma=False,
    )
```

```python
import jax
import jax.numpy as jnp
import numpy as np
from jax import lax
from jax.sharding import PartitionSpec as P
from jax.experimental import pallas as pl
from jax.experimental.pallas import tpu as pltpu

L = 21600
PA = 144
PB = 150
PH = 75


highest = lax.Precision.HIGHEST


def angle_table(first, second, period):
    phase = first * second % period
    return phase.astype(jnp.float32) * (2.0 * np.pi / period)


def forward_bands(grid, first_start, bands):
    rows = grid.shape[0]
    count_one = grid.shape[1]
    first_index = first_start + jnp.arange(count_one, dtype=jnp.int32)
    freq_one = jnp.arange(PA, dtype=jnp.int32)
    theta_one = angle_table(first_index[:, None], freq_one[None, :], PA)
    section_re = jnp.einsum("rab,ak->rbk", grid, jnp.cos(theta_one), precision=highest)
    section_im = -jnp.einsum("rab,ak->rbk", grid, jnp.sin(theta_one), precision=highest)
    second_index = jnp.arange(PB, dtype=jnp.int32)
    twist = angle_table(second_index[:, None], freq_one[None, :], L)
    twist_cos = jnp.cos(twist)
    twist_sin = jnp.sin(twist)
    turned_re = section_re * twist_cos + section_im * twist_sin
    turned_im = section_im * twist_cos - section_re * twist_sin
    freq_two = jnp.arange(PH, dtype=jnp.int32)
    theta_two = angle_table(second_index[:, None], freq_two[None, :], PB)
    cos_two = jnp.cos(theta_two)
    sin_two = jnp.sin(theta_two)
    spec_re = jnp.einsum("rbk,bm->rkm", turned_re, cos_two, precision=highest) + jnp.einsum(
        "rbk,bm->rkm", turned_im, sin_two, precision=highest
    )
    spec_im = jnp.einsum("rbk,bm->rkm", turned_im, cos_two, precision=highest) - jnp.einsum(
        "rbk,bm->rkm", turned_re, sin_two, precision=highest
    )
    scale = (2.0 / L) ** 0.5
    stacked = jnp.stack([spec_re, spec_im]) * scale
    span = PA // bands
    stacked = stacked.reshape(2, rows, span, bands, PH).transpose(3, 1, 0, 4, 2)
    return stacked.reshape(bands, rows, 2, PH * span)


def inverse_rows(spectra, band_ids, bands):
    count = spectra.shape[0]
    rows = spectra.shape[1]
    span = PA // bands
    parts = spectra.reshape(count, rows, 2, PH, span)
    part_re = parts[:, :, 0]
    part_im = parts[:, :, 1]
    freq_two = jnp.arange(PH, dtype=jnp.int32)
    second_index = jnp.arange(PB, dtype=jnp.int32)
    theta_two = angle_table(freq_two[:, None], second_index[None, :], PB)
    cos_two = jnp.cos(theta_two)
    sin_two = jnp.sin(theta_two)
    middle_re = jnp.einsum("brms,mn->brsn", part_re, cos_two, precision=highest) - jnp.einsum(
        "brms,mn->brsn", part_im, sin_two, precision=highest
    )
    middle_im = jnp.einsum("brms,mn->brsn", part_im, cos_two, precision=highest) + jnp.einsum(
        "brms,mn->brsn", part_re, sin_two, precision=highest
    )
    freq_one = jnp.arange(span, dtype=jnp.int32)[None, :] * bands + band_ids[:, None]
    twist = angle_table(freq_one[:, :, None], second_index[None, None, :], L)
    twist_cos = jnp.cos(twist)[:, None]
    twist_sin = jnp.sin(twist)[:, None]
    turned_re = middle_re * twist_cos - middle_im * twist_sin
    turned_im = middle_re * twist_sin + middle_im * twist_cos
    first_index = jnp.arange(PA, dtype=jnp.int32)
    theta_one = angle_table(freq_one[:, :, None], first_index[None, None, :], PA)
    grid = jnp.einsum(
        "brsn,bsa->ran", turned_re, jnp.cos(theta_one), precision=highest
    ) - jnp.einsum("brsn,bsa->ran", turned_im, jnp.sin(theta_one), precision=highest)
    return grid * (2.0 / L) ** 0.5


LANE = 128


def stokes_body(k_ref, w_ref, o_ref, sh_ref):
    shifts = sh_ref.shape[0]
    span = sh_ref.shape[1]
    steps = w_ref.shape[1] // shifts
    width = o_ref.shape[1]
    for r in range(shifts):
        sh_ref[r] = k_ref[pl.ds(r, span), :]

    def step(a, carry):
        acc_re, acc_im = carry
        base = pl.multiple_of(a * shifts, shifts)
        w_re = w_ref[0, pl.ds(base, shifts), :]
        w_im = w_ref[1, pl.ds(base, shifts), :]
        for r in range(shifts):
            slab = sh_ref[r, pl.ds(base, width), :]
            acc_re = acc_re + slab * w_re[r : r + 1, :]
            acc_im = acc_im + slab * w_im[r : r + 1, :]
        return acc_re, acc_im

    zero = jnp.zeros(o_ref.shape[1:], jnp.float32)
    acc_re, acc_im = lax.fori_loop(0, steps, step, (zero, zero))
    o_ref[0] = acc_re
    o_ref[1] = acc_im


def toeplitz_stokes(kernel, weighted, block_self, rows, blocks):
    total_rows = rows * blocks
    width = kernel.shape[1]
    padded = -(-width // LANE) * LANE
    shifts = 8
    everyone = lax.all_gather(weighted, "lat", axis=0, tiled=True)
    first = (blocks - 1 - block_self) * rows
    used = total_rows + rows - 1
    window = lax.dynamic_slice_in_dim(kernel, first, used, 0).astype(jnp.float32)
    window = jnp.pad(window, ((0, -used % shifts), (0, padded - width)))
    source = jnp.pad(
        everyone.astype(jnp.float32).transpose(1, 0, 2), ((0, 0), (0, 0), (0, padded - width))
    )
    span = total_rows + shifts
    out = pl.pallas_call(
        stokes_body,
        grid=(padded // LANE,),
        in_specs=[
            pl.BlockSpec((window.shape[0], LANE), lambda j: (0, j)),
            pl.BlockSpec((2, total_rows, LANE), lambda j: (0, 0, j)),
        ],
        out_specs=pl.BlockSpec((2, rows, LANE), lambda j: (0, 0, j)),
        out_shape=jax.ShapeDtypeStruct((2, rows, padded), jnp.float32),
        scratch_shapes=[pltpu.VMEM((shifts, span, LANE), jnp.float32)],
    )(window, source)
    return out[:, ::-1, :width].transpose(1, 0, 2)


def per_device(gravity, coef, legendre, order_table, band_rows, kernel):
    bands = lax.axis_size("freq")
    blocks = lax.axis_size("lat")
    band_self = lax.axis_index("freq")
    block_self = lax.axis_index("lat")
    rows = gravity.shape[0]
    whole_rows = lax.all_to_all(gravity, "freq", split_axis=0, concat_axis=1, tiled=True)
    terms = forward_bands(whole_rows.reshape(rows // bands, PA, PB), 0, bands)
    observed = lax.all_to_all(terms, "freq", split_axis=0, concat_axis=1, tiled=True)[0]
    band_width = observed.shape[2]
    synth = jnp.einsum("ocn,onq->ocq", coef, legendre, preferred_element_type=jnp.float32).astype(
        jnp.bfloat16
    )
    routed = lax.all_to_all(synth, "lat", split_axis=2, concat_axis=0, tiled=True)
    per_slot = coef.shape[0]
    slot_ids = (
        (jnp.arange(blocks, dtype=jnp.int32)[:, None] * bands + band_self) * per_slot
        + jnp.arange(per_slot, dtype=jnp.int32)[None, :]
    ).reshape(-1)
    positions = order_table[slot_ids] // bands
    selector = (positions[:, None] == jnp.arange(band_width, dtype=jnp.int32)[None, :]).astype(
        jnp.bfloat16
    )
    model = jnp.einsum("jcr,jt->rct", routed, selector, preferred_element_type=jnp.float32)
    weight = jnp.cos((20.0 + band_rows.astype(jnp.float32) / 60.0) * (np.pi / 180.0))
    weighted = ((observed - model) * weight[:, None, None]).astype(jnp.bfloat16)
    stokes = toeplitz_stokes(kernel, weighted, block_self, rows, blocks)
    by_band = lax.all_to_all(stokes[None], "freq", split_axis=1, concat_axis=0, tiled=True)
    grid_rows = inverse_rows(by_band, jnp.arange(bands, dtype=jnp.int32), bands)
    geoid = lax.all_to_all(grid_rows.reshape(rows // bands, L), "freq", split_axis=1, concat_axis=0, tiled=True)
    return geoid


def solution(mesh):
    return jax.shard_map(
        per_device,
        mesh=mesh,
        in_specs=(
            P("lat", "freq"),
            P(("lat", "freq"), None, None),
            P(("lat", "freq"), None, None),
            P(),
            P("lat"),
            P(None, "freq"),
        ),
        out_specs=P("lat", "freq"),
        check_vma=False,
    )
```

```python
import jax
import jax.numpy as jnp
import numpy as np
from jax import lax
from jax.sharding import PartitionSpec as P
from jax.experimental import pallas as pl
from jax.experimental.pallas import tpu as pltpu

L = 21600
PA = 144
PB = 150
PH = 75


highest = lax.Precision.HIGHEST


def angle_table(first, second, period):
    phase = first * second % period
    return phase.astype(jnp.float32) * (2.0 * np.pi / period)


def forward_bands(grid, first_start, bands):
    rows = grid.shape[0]
    count_one = grid.shape[1]
    first_index = first_start + jnp.arange(count_one, dtype=jnp.int32)
    freq_one = jnp.arange(PA, dtype=jnp.int32)
    theta_one = angle_table(first_index[:, None], freq_one[None, :], PA)
    section_re = jnp.einsum("rab,ak->rbk", grid, jnp.cos(theta_one), precision=highest)
    section_im = -jnp.einsum("rab,ak->rbk", grid, jnp.sin(theta_one), precision=highest)
    second_index = jnp.arange(PB, dtype=jnp.int32)
    twist = angle_table(second_index[:, None], freq_one[None, :], L)
    twist_cos = jnp.cos(twist)
    twist_sin = jnp.sin(twist)
    turned_re = section_re * twist_cos + section_im * twist_sin
    turned_im = section_im * twist_cos - section_re * twist_sin
    freq_two = jnp.arange(PH, dtype=jnp.int32)
    theta_two = angle_table(second_index[:, None], freq_two[None, :], PB)
    cos_two = jnp.cos(theta_two)
    sin_two = jnp.sin(theta_two)
    spec_re = jnp.einsum("rbk,bm->rkm", turned_re, cos_two, precision=highest) + jnp.einsum(
        "rbk,bm->rkm", turned_im, sin_two, precision=highest
    )
    spec_im = jnp.einsum("rbk,bm->rkm", turned_im, cos_two, precision=highest) - jnp.einsum(
        "rbk,bm->rkm", turned_re, sin_two, precision=highest
    )
    scale = (2.0 / L) ** 0.5
    stacked = jnp.stack([spec_re, spec_im]) * scale
    span = PA // bands
    stacked = stacked.reshape(2, rows, span, bands, PH).transpose(3, 1, 0, 4, 2)
    return stacked.reshape(bands, rows, 2, PH * span)


def inverse_rows(spectra, band_ids, bands):
    count = spectra.shape[0]
    rows = spectra.shape[1]
    span = PA // bands
    parts = spectra.reshape(count, rows, 2, PH, span)
    part_re = parts[:, :, 0]
    part_im = parts[:, :, 1]
    freq_two = jnp.arange(PH, dtype=jnp.int32)
    second_index = jnp.arange(PB, dtype=jnp.int32)
    theta_two = angle_table(freq_two[:, None], second_index[None, :], PB)
    cos_two = jnp.cos(theta_two)
    sin_two = jnp.sin(theta_two)
    middle_re = jnp.einsum("brms,mn->brsn", part_re, cos_two, precision=highest) - jnp.einsum(
        "brms,mn->brsn", part_im, sin_two, precision=highest
    )
    middle_im = jnp.einsum("brms,mn->brsn", part_im, cos_two, precision=highest) + jnp.einsum(
        "brms,mn->brsn", part_re, sin_two, precision=highest
    )
    freq_one = jnp.arange(span, dtype=jnp.int32)[None, :] * bands + band_ids[:, None]
    twist = angle_table(freq_one[:, :, None], second_index[None, None, :], L)
    twist_cos = jnp.cos(twist)[:, None]
    twist_sin = jnp.sin(twist)[:, None]
    turned_re = middle_re * twist_cos - middle_im * twist_sin
    turned_im = middle_re * twist_sin + middle_im * twist_cos
    first_index = jnp.arange(PA, dtype=jnp.int32)
    theta_one = angle_table(freq_one[:, :, None], first_index[None, None, :], PA)
    grid = jnp.einsum(
        "brsn,bsa->ran", turned_re, jnp.cos(theta_one), precision=highest
    ) - jnp.einsum("brsn,bsa->ran", turned_im, jnp.sin(theta_one), precision=highest)
    return grid * (2.0 / L) ** 0.5


LANE = 128
SHIFTS = 8
CHUNK = 64


def stokes_body(k_ref, w_ref, o_ref, sh_ref):
    span = sh_ref.shape[1]
    total = w_ref.shape[1]
    steps = total // SHIFTS
    for s in range(SHIFTS):
        sh_ref[s] = k_ref[pl.ds(s, span), :]
    for part in range(total // CHUNK):

        def step(a, carry):
            acc_re, acc_im = carry
            base = pl.multiple_of(a * SHIFTS, SHIFTS)
            w_re = w_ref[0, pl.ds(base, SHIFTS), :]
            w_im = w_ref[1, pl.ds(base, SHIFTS), :]
            start = pl.multiple_of(part * CHUNK + total - SHIFTS - base, SHIFTS)
            for r in range(SHIFTS):
                slab = sh_ref[SHIFTS - 1 - r, pl.ds(start, CHUNK), :]
                acc_re = acc_re + slab * w_re[r : r + 1, :]
                acc_im = acc_im + slab * w_im[r : r + 1, :]
            return acc_re, acc_im

        zero = jnp.zeros((CHUNK, LANE), jnp.float32)
        acc_re, acc_im = lax.fori_loop(0, steps, step, (zero, zero))
        o_ref[0, part * CHUNK : (part + 1) * CHUNK, :] = acc_re
        o_ref[1, part * CHUNK : (part + 1) * CHUNK, :] = acc_im


def toeplitz_stokes(kernel_cols, weighted):
    taps, width = kernel_cols.shape
    total = weighted.shape[0]
    span = 2 * total
    flipped = jnp.pad(
        kernel_cols[::-1].astype(jnp.float32), ((0, span + SHIFTS - taps), (0, LANE - width))
    )
    source = jnp.pad(weighted.astype(jnp.float32).transpose(1, 0, 2), ((0, 0), (0, 0), (0, LANE - width)))
    out = pl.pallas_call(
        stokes_body,
        out_shape=jax.ShapeDtypeStruct((2, total, LANE), jnp.float32),
        scratch_shapes=[pltpu.VMEM((SHIFTS, span, LANE), jnp.float32)],
    )(flipped, source)
    return out[:, :, :width]


def per_device(gravity, coef, legendre, order_table, band_rows, kernel):
    bands = lax.axis_size("freq")
    blocks = lax.axis_size("lat")
    band_self = lax.axis_index("freq")
    block_self = lax.axis_index("lat")
    everyone = ("lat", "freq")
    devices = bands * blocks
    rows = gravity.shape[0]
    total_rows = rows * blocks
    mine = rows // bands
    band_width = kernel.shape[1]
    sub = -(-band_width // blocks)
    padded = sub * blocks
    whole_rows = lax.all_to_all(gravity, "freq", split_axis=0, concat_axis=1, tiled=True)
    terms = forward_bands(whole_rows.reshape(mine, PA, PB), 0, bands)
    terms = jnp.pad(terms, ((0, 0), (0, 0), (0, 0), (0, padded - band_width)))
    terms = terms.reshape(bands, mine, 2, blocks, sub).transpose(3, 0, 1, 2, 4)
    terms = terms.reshape(devices, mine, 2, sub)
    observed = lax.all_to_all(terms, everyone, split_axis=0, concat_axis=0, tiled=True)
    observed = observed.reshape(total_rows, 2, sub)
    synth = jnp.einsum("ocn,onq->ocq", coef, legendre, preferred_element_type=jnp.float32).astype(
        jnp.bfloat16
    )
    routed = lax.all_gather(synth, "lat", axis=0, tiled=True)
    per_slot = coef.shape[0]
    slot_ids = (
        (jnp.arange(blocks, dtype=jnp.int32)[:, None] * bands + band_self) * per_slot
        + jnp.arange(per_slot, dtype=jnp.int32)[None, :]
    ).reshape(-1)
    positions = order_table[slot_ids] // bands - block_self * sub
    selector = (positions[:, None] == jnp.arange(sub, dtype=jnp.int32)[None, :]).astype(
        jnp.bfloat16
    )
    model = jnp.einsum("jcr,jt->rct", routed, selector, preferred_element_type=jnp.float32)
    all_rows = lax.all_gather(band_rows, "lat", axis=0, tiled=True)
    weight = jnp.cos((20.0 + all_rows.astype(jnp.float32) / 60.0) * (np.pi / 180.0))
    weighted = ((observed - model) * weight[:, None, None]).astype(jnp.bfloat16)
    kernel_cols = lax.dynamic_slice_in_dim(
        jnp.pad(kernel, ((0, 0), (0, padded - band_width))), block_self * sub, sub, 1
    )
    stokes = toeplitz_stokes(kernel_cols, weighted)
    stokes = stokes.reshape(2, devices, mine, sub).transpose(1, 2, 0, 3)
    by_source = lax.all_to_all(stokes, everyone, split_axis=0, concat_axis=0, tiled=True)
    by_band = by_source.reshape(blocks, bands, mine, 2, sub).transpose(1, 2, 3, 0, 4)
    by_band = by_band.reshape(bands, mine, 2, padded)[..., :band_width]
    grid_rows = inverse_rows(by_band, jnp.arange(bands, dtype=jnp.int32), bands)
    geoid = lax.all_to_all(grid_rows.reshape(mine, L), "freq", split_axis=1, concat_axis=0, tiled=True)
    return geoid


def solution(mesh):
    return jax.shard_map(
        per_device,
        mesh=mesh,
        in_specs=(
            P("lat", "freq"),
            P(("lat", "freq"), None, None),
            P(("lat", "freq"), None, None),
            P(),
            P("lat"),
            P(None, "freq"),
        ),
        out_specs=P("lat", "freq"),
        check_vma=False,
    )
```

```python
import jax
import jax.numpy as jnp
import numpy as np
from jax import lax
from jax.sharding import PartitionSpec as P
from jax.experimental import pallas as pl
from jax.experimental.pallas import tpu as pltpu

L = 21600
PA = 144
PB = 150
PH = 75


highest = lax.Precision.HIGHEST


def angle_table(first, second, period):
    phase = first * second % period
    return phase.astype(jnp.float32) * (2.0 * np.pi / period)


def forward_bands(grid, first_start, bands):
    rows = grid.shape[0]
    count_one = grid.shape[1]
    first_index = first_start + jnp.arange(count_one, dtype=jnp.int32)
    freq_one = jnp.arange(PA, dtype=jnp.int32)
    theta_one = angle_table(first_index[:, None], freq_one[None, :], PA)
    section_re = jnp.einsum("rab,ak->rbk", grid, jnp.cos(theta_one), precision=highest)
    section_im = -jnp.einsum("rab,ak->rbk", grid, jnp.sin(theta_one), precision=highest)
    second_index = jnp.arange(PB, dtype=jnp.int32)
    twist = angle_table(second_index[:, None], freq_one[None, :], L)
    twist_cos = jnp.cos(twist)
    twist_sin = jnp.sin(twist)
    turned_re = section_re * twist_cos + section_im * twist_sin
    turned_im = section_im * twist_cos - section_re * twist_sin
    freq_two = jnp.arange(PH, dtype=jnp.int32)
    theta_two = angle_table(second_index[:, None], freq_two[None, :], PB)
    cos_two = jnp.cos(theta_two)
    sin_two = jnp.sin(theta_two)
    spec_re = jnp.einsum("rbk,bm->rkm", turned_re, cos_two, precision=highest) + jnp.einsum(
        "rbk,bm->rkm", turned_im, sin_two, precision=highest
    )
    spec_im = jnp.einsum("rbk,bm->rkm", turned_im, cos_two, precision=highest) - jnp.einsum(
        "rbk,bm->rkm", turned_re, sin_two, precision=highest
    )
    scale = (2.0 / L) ** 0.5
    stacked = jnp.stack([spec_re, spec_im]) * scale
    span = PA // bands
    stacked = stacked.reshape(2, rows, span, bands, PH).transpose(3, 1, 0, 4, 2)
    return stacked.reshape(bands, rows, 2, PH * span)


def inverse_rows(spectra, band_ids, bands):
    count = spectra.shape[0]
    rows = spectra.shape[1]
    span = PA // bands
    parts = spectra.reshape(count, rows, 2, PH, span)
    part_re = parts[:, :, 0]
    part_im = parts[:, :, 1]
    freq_two = jnp.arange(PH, dtype=jnp.int32)
    second_index = jnp.arange(PB, dtype=jnp.int32)
    theta_two = angle_table(freq_two[:, None], second_index[None, :], PB)
    cos_two = jnp.cos(theta_two)
    sin_two = jnp.sin(theta_two)
    middle_re = jnp.einsum("brms,mn->brsn", part_re, cos_two, precision=highest) - jnp.einsum(
        "brms,mn->brsn", part_im, sin_two, precision=highest
    )
    middle_im = jnp.einsum("brms,mn->brsn", part_im, cos_two, precision=highest) + jnp.einsum(
        "brms,mn->brsn", part_re, sin_two, precision=highest
    )
    freq_one = jnp.arange(span, dtype=jnp.int32)[None, :] * bands + band_ids[:, None]
    twist = angle_table(freq_one[:, :, None], second_index[None, None, :], L)
    twist_cos = jnp.cos(twist)[:, None]
    twist_sin = jnp.sin(twist)[:, None]
    turned_re = middle_re * twist_cos - middle_im * twist_sin
    turned_im = middle_re * twist_sin + middle_im * twist_cos
    first_index = jnp.arange(PA, dtype=jnp.int32)
    theta_one = angle_table(freq_one[:, :, None], first_index[None, None, :], PA)
    grid = jnp.einsum(
        "brsn,bsa->ran", turned_re, jnp.cos(theta_one), precision=highest
    ) - jnp.einsum("brsn,bsa->ran", turned_im, jnp.sin(theta_one), precision=highest)
    return grid * (2.0 / L) ** 0.5


LANE = 128
SHIFTS = 8
CHUNK = 64


def stokes_body(k_ref, w_ref, o_ref, sh_ref):
    span = sh_ref.shape[1]
    total = w_ref.shape[1]
    steps = total // SHIFTS
    for s in range(SHIFTS):
        sh_ref[s] = k_ref[pl.ds(s, span), :]
    for part in range(total // CHUNK):

        def step(a, carry):
            acc_re, acc_im = carry
            base = pl.multiple_of(a * SHIFTS, SHIFTS)
            w_re = w_ref[0, pl.ds(base, SHIFTS), :]
            w_im = w_ref[1, pl.ds(base, SHIFTS), :]
            start = pl.multiple_of(part * CHUNK + total - SHIFTS - base, SHIFTS)
            for r in range(SHIFTS):
                slab = sh_ref[SHIFTS - 1 - r, pl.ds(start, CHUNK), :]
                acc_re = acc_re + slab * w_re[r : r + 1, :]
                acc_im = acc_im + slab * w_im[r : r + 1, :]
            return acc_re, acc_im

        zero = jnp.zeros((CHUNK, LANE), jnp.float32)
        acc_re, acc_im = lax.fori_loop(0, steps, step, (zero, zero))
        o_ref[0, part * CHUNK : (part + 1) * CHUNK, :] = acc_re
        o_ref[1, part * CHUNK : (part + 1) * CHUNK, :] = acc_im


def toeplitz_stokes(kernel_cols, weighted):
    taps, width = kernel_cols.shape
    total = weighted.shape[0]
    span = 2 * total
    flipped = jnp.pad(
        kernel_cols[::-1].astype(jnp.float32), ((0, span + SHIFTS - taps), (0, LANE - width))
    )
    source = jnp.pad(weighted.astype(jnp.float32).transpose(1, 0, 2), ((0, 0), (0, 0), (0, LANE - width)))
    out = pl.pallas_call(
        stokes_body,
        out_shape=jax.ShapeDtypeStruct((2, total, LANE), jnp.float32),
        scratch_shapes=[pltpu.VMEM((SHIFTS, span, LANE), jnp.float32)],
    )(flipped, source)
    return out[:, :, :width]


def per_device(gravity, coef, legendre, order_table, band_rows, kernel):
    bands = lax.axis_size("freq")
    blocks = lax.axis_size("lat")
    band_self = lax.axis_index("freq")
    block_self = lax.axis_index("lat")
    everyone = ("lat", "freq")
    devices = bands * blocks
    rows = gravity.shape[0]
    total_rows = rows * blocks
    mine = rows // bands
    band_width = kernel.shape[1]
    sub = -(-band_width // blocks)
    padded = sub * blocks
    whole_rows = lax.all_to_all(gravity, "freq", split_axis=0, concat_axis=1, tiled=True)
    terms = forward_bands(whole_rows.reshape(mine, PA, PB), 0, bands)
    synth = jnp.einsum("ocn,onq->ocq", coef, legendre, preferred_element_type=jnp.float32).astype(
        jnp.bfloat16
    )
    per_slot = coef.shape[0]
    held = blocks * per_slot
    routed = lax.all_to_all(
        synth.reshape(per_slot, 2, devices, mine), everyone, split_axis=2, concat_axis=0, tiled=True
    )
    routed = routed.reshape(blocks, bands, per_slot, 2, mine).transpose(1, 0, 2, 3, 4)
    routed = routed.reshape(bands, held, 2, mine)
    positions = order_table.reshape(blocks, bands, per_slot).transpose(1, 0, 2).reshape(bands, held)
    selector = (
        positions[:, :, None] // bands == jnp.arange(held, dtype=jnp.int32)[None, None, :]
    ).astype(jnp.bfloat16)
    model = jnp.einsum("bjcr,bjt->brct", routed, selector, preferred_element_type=jnp.float32)
    model = jnp.pad(model, ((0, 0), (0, 0), (0, 0), (0, band_width - held)))
    my_rows = lax.dynamic_slice_in_dim(band_rows, band_self * mine, mine, 0)
    weight = jnp.cos((20.0 + my_rows.astype(jnp.float32) / 60.0) * (np.pi / 180.0))
    weighted = ((terms - model) * weight[None, :, None, None]).astype(jnp.bfloat16)
    weighted = jnp.pad(weighted, ((0, 0), (0, 0), (0, 0), (0, padded - band_width)))
    weighted = weighted.reshape(bands, mine, 2, blocks, sub).transpose(3, 0, 1, 2, 4)
    weighted = weighted.reshape(devices, mine, 2, sub)
    weighted = lax.all_to_all(weighted, everyone, split_axis=0, concat_axis=0, tiled=True)
    weighted = weighted.reshape(total_rows, 2, sub)
    kernel_cols = lax.dynamic_slice_in_dim(
        jnp.pad(kernel, ((0, 0), (0, padded - band_width))), block_self * sub, sub, 1
    )
    stokes = toeplitz_stokes(kernel_cols, weighted)
    stokes = stokes.reshape(2, devices, mine, sub).transpose(1, 2, 0, 3)
    by_source = lax.all_to_all(stokes, everyone, split_axis=0, concat_axis=0, tiled=True)
    by_band = by_source.reshape(blocks, bands, mine, 2, sub).transpose(1, 2, 3, 0, 4)
    by_band = by_band.reshape(bands, mine, 2, padded)[..., :band_width]
    grid_rows = inverse_rows(by_band, jnp.arange(bands, dtype=jnp.int32), bands)
    geoid = lax.all_to_all(grid_rows.reshape(mine, L), "freq", split_axis=1, concat_axis=0, tiled=True)
    return geoid


def solution(mesh):
    return jax.shard_map(
        per_device,
        mesh=mesh,
        in_specs=(
            P("lat", "freq"),
            P(("lat", "freq"), None, None),
            P(("lat", "freq"), None, None),
            P(),
            P("lat"),
            P(None, "freq"),
        ),
        out_specs=P("lat", "freq"),
        check_vma=False,
    )
```

```python
import jax
import jax.numpy as jnp
import numpy as np
from jax import lax
from jax.sharding import PartitionSpec as P
from jax.experimental import pallas as pl
from jax.experimental.pallas import tpu as pltpu

L = 21600
PA = 144
PB = 150
PH = 75


highest = lax.Precision.HIGHEST


def angle_table(first, second, period):
    phase = first * second % period
    return phase.astype(jnp.float32) * (2.0 * np.pi / period)


def forward_bands(grid, first_start, bands):
    rows = grid.shape[0]
    count_one = grid.shape[1]
    first_index = first_start + jnp.arange(count_one, dtype=jnp.int32)
    freq_one = jnp.arange(PA, dtype=jnp.int32)
    theta_one = angle_table(first_index[:, None], freq_one[None, :], PA)
    section_re = jnp.einsum("rab,ak->rbk", grid, jnp.cos(theta_one), precision=highest)
    section_im = -jnp.einsum("rab,ak->rbk", grid, jnp.sin(theta_one), precision=highest)
    second_index = jnp.arange(PB, dtype=jnp.int32)
    twist = angle_table(second_index[:, None], freq_one[None, :], L)
    twist_cos = jnp.cos(twist)
    twist_sin = jnp.sin(twist)
    turned_re = section_re * twist_cos + section_im * twist_sin
    turned_im = section_im * twist_cos - section_re * twist_sin
    freq_two = jnp.arange(PH, dtype=jnp.int32)
    theta_two = angle_table(second_index[:, None], freq_two[None, :], PB)
    cos_two = jnp.cos(theta_two)
    sin_two = jnp.sin(theta_two)
    spec_re = jnp.einsum("rbk,bm->rkm", turned_re, cos_two, precision=highest) + jnp.einsum(
        "rbk,bm->rkm", turned_im, sin_two, precision=highest
    )
    spec_im = jnp.einsum("rbk,bm->rkm", turned_im, cos_two, precision=highest) - jnp.einsum(
        "rbk,bm->rkm", turned_re, sin_two, precision=highest
    )
    scale = (2.0 / L) ** 0.5
    stacked = jnp.stack([spec_re, spec_im]) * scale
    span = PA // bands
    stacked = stacked.reshape(2, rows, span, bands, PH).transpose(3, 1, 0, 4, 2)
    return stacked.reshape(bands, rows, 2, PH * span)


def inverse_rows(spectra, band_ids, bands):
    count = spectra.shape[0]
    rows = spectra.shape[1]
    span = PA // bands
    parts = spectra.reshape(count, rows, 2, PH, span)
    part_re = parts[:, :, 0]
    part_im = parts[:, :, 1]
    freq_two = jnp.arange(PH, dtype=jnp.int32)
    second_index = jnp.arange(PB, dtype=jnp.int32)
    theta_two = angle_table(freq_two[:, None], second_index[None, :], PB)
    cos_two = jnp.cos(theta_two)
    sin_two = jnp.sin(theta_two)
    middle_re = jnp.einsum("brms,mn->brsn", part_re, cos_two, precision=highest) - jnp.einsum(
        "brms,mn->brsn", part_im, sin_two, precision=highest
    )
    middle_im = jnp.einsum("brms,mn->brsn", part_im, cos_two, precision=highest) + jnp.einsum(
        "brms,mn->brsn", part_re, sin_two, precision=highest
    )
    freq_one = jnp.arange(span, dtype=jnp.int32)[None, :] * bands + band_ids[:, None]
    twist = angle_table(freq_one[:, :, None], second_index[None, None, :], L)
    twist_cos = jnp.cos(twist)[:, None]
    twist_sin = jnp.sin(twist)[:, None]
    turned_re = middle_re * twist_cos - middle_im * twist_sin
    turned_im = middle_re * twist_sin + middle_im * twist_cos
    first_index = jnp.arange(PA, dtype=jnp.int32)
    theta_one = angle_table(freq_one[:, :, None], first_index[None, None, :], PA)
    grid = jnp.einsum(
        "brsn,bsa->ran", turned_re, jnp.cos(theta_one), precision=highest
    ) - jnp.einsum("brsn,bsa->ran", turned_im, jnp.sin(theta_one), precision=highest)
    return grid * (2.0 / L) ** 0.5


LANE = 128
SHIFTS = 8
CHUNK = 64


def stokes_body(k_ref, w_ref, o_ref, sh_ref):
    span = sh_ref.shape[1]
    total = w_ref.shape[1]
    steps = total // SHIFTS
    for s in range(SHIFTS):
        sh_ref[s] = k_ref[pl.ds(s, span), :]
    for part in range(total // CHUNK):

        def step(a, carry):
            acc_re, acc_im = carry
            base = pl.multiple_of(a * SHIFTS, SHIFTS)
            w_re = w_ref[0, pl.ds(base, SHIFTS), :]
            w_im = w_ref[1, pl.ds(base, SHIFTS), :]
            start = pl.multiple_of(part * CHUNK + total - SHIFTS - base, SHIFTS)
            for r in range(SHIFTS):
                slab = sh_ref[SHIFTS - 1 - r, pl.ds(start, CHUNK), :]
                acc_re = acc_re + slab * w_re[r : r + 1, :]
                acc_im = acc_im + slab * w_im[r : r + 1, :]
            return acc_re, acc_im

        zero = jnp.zeros((CHUNK, LANE), jnp.float32)
        acc_re, acc_im = lax.fori_loop(0, steps, step, (zero, zero))
        o_ref[0, part * CHUNK : (part + 1) * CHUNK, :] = acc_re
        o_ref[1, part * CHUNK : (part + 1) * CHUNK, :] = acc_im


def toeplitz_stokes(kernel_cols, weighted):
    taps, width = kernel_cols.shape
    total = weighted.shape[0]
    span = 2 * total
    flipped = jnp.pad(
        kernel_cols[::-1].astype(jnp.float32), ((0, span + SHIFTS - taps), (0, LANE - width))
    )
    source = jnp.pad(weighted.astype(jnp.float32).transpose(1, 0, 2), ((0, 0), (0, 0), (0, LANE - width)))
    out = pl.pallas_call(
        stokes_body,
        out_shape=jax.ShapeDtypeStruct((2, total, LANE), jnp.float32),
        scratch_shapes=[pltpu.VMEM((SHIFTS, span, LANE), jnp.float32)],
    )(flipped, source)
    return out[:, :, :width]


def per_device(gravity, coef, legendre, order_table, band_rows, kernel):
    bands = lax.axis_size("freq")
    blocks = lax.axis_size("lat")
    band_self = lax.axis_index("freq")
    block_self = lax.axis_index("lat")
    everyone = ("lat", "freq")
    devices = bands * blocks
    rows = gravity.shape[0]
    total_rows = rows * blocks
    mine = rows // bands
    band_width = kernel.shape[1]
    per_slot = coef.shape[0]
    held = blocks * per_slot
    sub = -(-band_width // blocks)
    share = sub - per_slot
    padded = held + share * blocks
    positions = order_table.reshape(blocks, bands, per_slot).transpose(1, 0, 2).reshape(bands, held) // bands
    slot_of = jnp.sum(
        jnp.where(
            positions[:, :, None] == jnp.arange(held, dtype=jnp.int32)[None, None, :],
            jnp.arange(held, dtype=jnp.int32)[None, :, None],
            0,
        ),
        axis=1,
    )

    whole_rows = lax.all_to_all(gravity, "freq", split_axis=0, concat_axis=1, tiled=True)
    terms = forward_bands(whole_rows.reshape(mine, PA, PB), 0, bands)
    own = jnp.take_along_axis(terms[..., :held], positions[:, None, None, :], axis=3)
    own = own.reshape(bands, mine, 2, blocks, per_slot)
    rest = jnp.pad(terms[..., held:], ((0, 0), (0, 0), (0, 0), (0, padded - band_width)))
    rest = rest.reshape(bands, mine, 2, blocks, share)
    my_rows = lax.dynamic_slice_in_dim(band_rows, band_self * mine, mine, 0)
    weight = jnp.cos((20.0 + my_rows.astype(jnp.float32) / 60.0) * (np.pi / 180.0))
    carried = jnp.broadcast_to(weight[None, :, None, None, None], (bands, mine, 2, blocks, 1))
    payload = jnp.concatenate([own, rest, carried], axis=4).transpose(3, 0, 1, 2, 4)
    payload = payload.reshape(devices, mine, 2, sub + 1)
    observed = lax.all_to_all(payload, everyone, split_axis=0, concat_axis=0, tiled=True)
    observed = observed.reshape(total_rows, 2, sub + 1)
    weight_all = observed[:, 0, sub]
    observed = observed[:, :, :sub]

    synth = jnp.einsum("ocn,onq->ocq", coef, legendre, preferred_element_type=jnp.float32).astype(
        jnp.bfloat16
    )
    model = jnp.pad(synth.astype(jnp.float32).transpose(2, 1, 0), ((0, 0), (0, 0), (0, share)))
    weighted = ((observed - model) * weight_all[:, None, None]).astype(jnp.bfloat16)

    own_cols = lax.dynamic_slice_in_dim(positions[band_self], block_self * per_slot, per_slot, 0)
    kernel_own = jnp.take(kernel, own_cols, axis=1)
    kernel_rest = lax.dynamic_slice_in_dim(
        jnp.pad(kernel, ((0, 0), (0, padded - band_width))), held + block_self * share, share, 1
    )
    stokes = toeplitz_stokes(jnp.concatenate([kernel_own, kernel_rest], axis=1), weighted)
    stokes = stokes.reshape(2, devices, mine, sub).transpose(1, 2, 0, 3)
    by_source = lax.all_to_all(stokes, everyone, split_axis=0, concat_axis=0, tiled=True)
    by_source = by_source.reshape(blocks, bands, mine, 2, sub).transpose(1, 2, 3, 0, 4)
    slots_back = by_source[..., :per_slot].reshape(bands, mine, 2, held)
    slots_back = jnp.take_along_axis(slots_back, slot_of[:, None, None, :], axis=3)
    rest_back = by_source[..., per_slot:].reshape(bands, mine, 2, blocks * share)
    by_band = jnp.concatenate([slots_back, rest_back], axis=3)[..., :band_width]
    grid_rows = inverse_rows(by_band, jnp.arange(bands, dtype=jnp.int32), bands)
    geoid = lax.all_to_all(grid_rows.reshape(mine, L), "freq", split_axis=1, concat_axis=0, tiled=True)
    return geoid


def solution(mesh):
    return jax.shard_map(
        per_device,
        mesh=mesh,
        in_specs=(
            P("lat", "freq"),
            P(("lat", "freq"), None, None),
            P(("lat", "freq"), None, None),
            P(),
            P("lat"),
            P(None, "freq"),
        ),
        out_specs=P("lat", "freq"),
        check_vma=False,
    )
```

```python
import jax
import jax.numpy as jnp
import numpy as np
from jax import lax
from jax.sharding import PartitionSpec as P
from jax.experimental import pallas as pl
from jax.experimental.pallas import tpu as pltpu

L = 21600
PA = 144
PB = 150
PH = 75


highest = lax.Precision.HIGHEST


def angle_table(first, second, period):
    phase = first * second % period
    return phase.astype(jnp.float32) * (2.0 * np.pi / period)


def forward_bands(grid, first_start, bands):
    rows = grid.shape[0]
    count_one = grid.shape[1]
    first_index = first_start + jnp.arange(count_one, dtype=jnp.int32)
    freq_one = jnp.arange(PA, dtype=jnp.int32)
    theta_one = angle_table(first_index[:, None], freq_one[None, :], PA)
    section_re = jnp.einsum("rab,ak->rbk", grid, jnp.cos(theta_one), precision=highest)
    section_im = -jnp.einsum("rab,ak->rbk", grid, jnp.sin(theta_one), precision=highest)
    second_index = jnp.arange(PB, dtype=jnp.int32)
    twist = angle_table(second_index[:, None], freq_one[None, :], L)
    twist_cos = jnp.cos(twist)
    twist_sin = jnp.sin(twist)
    turned_re = section_re * twist_cos + section_im * twist_sin
    turned_im = section_im * twist_cos - section_re * twist_sin
    freq_two = jnp.arange(PH, dtype=jnp.int32)
    theta_two = angle_table(second_index[:, None], freq_two[None, :], PB)
    cos_two = jnp.cos(theta_two)
    sin_two = jnp.sin(theta_two)
    spec_re = jnp.einsum("rbk,bm->rkm", turned_re, cos_two, precision=highest) + jnp.einsum(
        "rbk,bm->rkm", turned_im, sin_two, precision=highest
    )
    spec_im = jnp.einsum("rbk,bm->rkm", turned_im, cos_two, precision=highest) - jnp.einsum(
        "rbk,bm->rkm", turned_re, sin_two, precision=highest
    )
    scale = (2.0 / L) ** 0.5
    stacked = jnp.stack([spec_re, spec_im]) * scale
    span = PA // bands
    stacked = stacked.reshape(2, rows, span, bands, PH).transpose(3, 1, 0, 4, 2)
    return stacked.reshape(bands, rows, 2, PH * span)


def inverse_rows(spectra, band_ids, bands):
    count = spectra.shape[0]
    rows = spectra.shape[1]
    span = PA // bands
    parts = spectra.reshape(count, rows, 2, PH, span)
    part_re = parts[:, :, 0]
    part_im = parts[:, :, 1]
    freq_two = jnp.arange(PH, dtype=jnp.int32)
    second_index = jnp.arange(PB, dtype=jnp.int32)
    theta_two = angle_table(freq_two[:, None], second_index[None, :], PB)
    cos_two = jnp.cos(theta_two)
    sin_two = jnp.sin(theta_two)
    middle_re = jnp.einsum("brms,mn->brsn", part_re, cos_two, precision=highest) - jnp.einsum(
        "brms,mn->brsn", part_im, sin_two, precision=highest
    )
    middle_im = jnp.einsum("brms,mn->brsn", part_im, cos_two, precision=highest) + jnp.einsum(
        "brms,mn->brsn", part_re, sin_two, precision=highest
    )
    freq_one = jnp.arange(span, dtype=jnp.int32)[None, :] * bands + band_ids[:, None]
    twist = angle_table(freq_one[:, :, None], second_index[None, None, :], L)
    twist_cos = jnp.cos(twist)[:, None]
    twist_sin = jnp.sin(twist)[:, None]
    turned_re = middle_re * twist_cos - middle_im * twist_sin
    turned_im = middle_re * twist_sin + middle_im * twist_cos
    first_index = jnp.arange(PA, dtype=jnp.int32)
    theta_one = angle_table(freq_one[:, :, None], first_index[None, None, :], PA)
    grid = jnp.einsum(
        "brsn,bsa->ran", turned_re, jnp.cos(theta_one), precision=highest
    ) - jnp.einsum("brsn,bsa->ran", turned_im, jnp.sin(theta_one), precision=highest)
    return grid * (2.0 / L) ** 0.5


LANE = 128
SHIFTS = 8
CHUNK = 64


def stokes_body(k_ref, w_ref, o_ref, sh_ref):
    span = sh_ref.shape[1]
    total = w_ref.shape[1]
    steps = total // SHIFTS
    for s in range(SHIFTS):
        sh_ref[s] = k_ref[pl.ds(s, span), :]
    for part in range(total // CHUNK):

        def step(a, carry):
            acc_re, acc_im = carry
            base = pl.multiple_of(a * SHIFTS, SHIFTS)
            w_re = w_ref[0, pl.ds(base, SHIFTS), :]
            w_im = w_ref[1, pl.ds(base, SHIFTS), :]
            start = pl.multiple_of(part * CHUNK + total - SHIFTS - base, SHIFTS)
            for r in range(SHIFTS):
                slab = sh_ref[SHIFTS - 1 - r, pl.ds(start, CHUNK), :]
                acc_re = acc_re + slab * w_re[r : r + 1, :]
                acc_im = acc_im + slab * w_im[r : r + 1, :]
            return acc_re, acc_im

        zero = jnp.zeros((CHUNK, LANE), jnp.float32)
        acc_re, acc_im = lax.fori_loop(0, steps, step, (zero, zero))
        o_ref[0, part * CHUNK : (part + 1) * CHUNK, :] = acc_re
        o_ref[1, part * CHUNK : (part + 1) * CHUNK, :] = acc_im


def toeplitz_stokes(kernel_cols, weighted):
    taps, width = kernel_cols.shape
    total = weighted.shape[0]
    span = 2 * total
    flipped = jnp.pad(
        kernel_cols[::-1].astype(jnp.float32), ((0, span + SHIFTS - taps), (0, LANE - width))
    )
    source = jnp.pad(weighted.astype(jnp.float32).transpose(1, 0, 2), ((0, 0), (0, 0), (0, LANE - width)))
    out = pl.pallas_call(
        stokes_body,
        out_shape=jax.ShapeDtypeStruct((2, total, LANE), jnp.float32),
        scratch_shapes=[pltpu.VMEM((SHIFTS, span, LANE), jnp.float32)],
    )(flipped, source)
    return out[:, :, :width]


def per_device(gravity, coef, legendre, order_table, band_rows, kernel):
    bands = lax.axis_size("freq")
    blocks = lax.axis_size("lat")
    band_self = lax.axis_index("freq")
    block_self = lax.axis_index("lat")
    everyone = ("lat", "freq")
    devices = bands * blocks
    rows = gravity.shape[0]
    total_rows = rows * blocks
    mine = rows // bands
    band_width = kernel.shape[1]
    per_slot = coef.shape[0]
    held = blocks * per_slot
    sub = -(-band_width // blocks)
    share = sub - per_slot
    padded = held + share * blocks
    positions = order_table.reshape(blocks, bands, per_slot).transpose(1, 0, 2).reshape(bands, held) // bands
    selector = (
        positions[:, None, :] == jnp.arange(held, dtype=jnp.int32)[None, :, None]
    ).astype(jnp.float32)

    whole_rows = lax.all_to_all(gravity, "freq", split_axis=0, concat_axis=1, tiled=True)
    terms = forward_bands(whole_rows.reshape(mine, PA, PB), 0, bands)
    own = jnp.einsum("brct,bts->brcs", terms[..., :held], selector, precision=highest)
    own = own.reshape(bands, mine, 2, blocks, per_slot)
    rest = jnp.pad(terms[..., held:], ((0, 0), (0, 0), (0, 0), (0, padded - band_width)))
    rest = rest.reshape(bands, mine, 2, blocks, share)
    my_rows = lax.dynamic_slice_in_dim(band_rows, band_self * mine, mine, 0)
    weight = jnp.cos((20.0 + my_rows.astype(jnp.float32) / 60.0) * (np.pi / 180.0))
    carried = jnp.broadcast_to(weight[None, :, None, None, None], (bands, mine, 2, blocks, 1))
    payload = jnp.concatenate([own, rest, carried], axis=4).transpose(3, 0, 1, 2, 4)
    payload = payload.reshape(devices, mine, 2, sub + 1)
    observed = lax.all_to_all(payload, everyone, split_axis=0, concat_axis=0, tiled=True)
    observed = observed.reshape(total_rows, 2, sub + 1)
    weight_all = observed[:, 0, sub]
    observed = observed[:, :, :sub]

    synth = jnp.einsum("ocn,onq->ocq", coef, legendre, preferred_element_type=jnp.float32).astype(
        jnp.bfloat16
    )
    model = jnp.pad(synth.astype(jnp.float32).transpose(2, 1, 0), ((0, 0), (0, 0), (0, share)))
    weighted = ((observed - model) * weight_all[:, None, None]).astype(jnp.bfloat16)

    own_cols = lax.dynamic_slice_in_dim(positions[band_self], block_self * per_slot, per_slot, 0)
    kernel_own = jnp.take(kernel, own_cols, axis=1)
    kernel_rest = lax.dynamic_slice_in_dim(
        jnp.pad(kernel, ((0, 0), (0, padded - band_width))), held + block_self * share, share, 1
    )
    stokes = toeplitz_stokes(jnp.concatenate([kernel_own, kernel_rest], axis=1), weighted)
    stokes = stokes.reshape(2, devices, mine, sub).transpose(1, 2, 0, 3)
    by_source = lax.all_to_all(stokes, everyone, split_axis=0, concat_axis=0, tiled=True)
    by_source = by_source.reshape(blocks, bands, mine, 2, sub).transpose(1, 2, 3, 0, 4)
    slots_back = by_source[..., :per_slot].reshape(bands, mine, 2, held)
    slots_back = jnp.einsum("brcs,bts->brct", slots_back, selector, precision=highest)
    rest_back = by_source[..., per_slot:].reshape(bands, mine, 2, blocks * share)
    by_band = jnp.concatenate([slots_back, rest_back], axis=3)[..., :band_width]
    grid_rows = inverse_rows(by_band, jnp.arange(bands, dtype=jnp.int32), bands)
    geoid = lax.all_to_all(grid_rows.reshape(mine, L), "freq", split_axis=1, concat_axis=0, tiled=True)
    return geoid


def solution(mesh):
    return jax.shard_map(
        per_device,
        mesh=mesh,
        in_specs=(
            P("lat", "freq"),
            P(("lat", "freq"), None, None),
            P(("lat", "freq"), None, None),
            P(),
            P("lat"),
            P(None, "freq"),
        ),
        out_specs=P("lat", "freq"),
        check_vma=False,
    )
```

```python
import jax
import jax.numpy as jnp
import numpy as np
from jax import lax
from jax.sharding import PartitionSpec as P
from jax.experimental import pallas as pl
from jax.experimental.pallas import tpu as pltpu

L = 21600
PA = 144
PB = 150
PH = 75


highest = lax.Precision.HIGHEST


def angle_table(first, second, period):
    phase = first * second % period
    return phase.astype(jnp.float32) * (2.0 * np.pi / period)


def forward_bands(grid, first_start, bands):
    rows = grid.shape[0]
    count_one = grid.shape[1]
    first_index = first_start + jnp.arange(count_one, dtype=jnp.int32)
    freq_one = jnp.arange(PA, dtype=jnp.int32)
    theta_one = angle_table(first_index[:, None], freq_one[None, :], PA)
    section_re = jnp.einsum("rab,ak->rbk", grid, jnp.cos(theta_one), precision=highest)
    section_im = -jnp.einsum("rab,ak->rbk", grid, jnp.sin(theta_one), precision=highest)
    second_index = jnp.arange(PB, dtype=jnp.int32)
    twist = angle_table(second_index[:, None], freq_one[None, :], L)
    twist_cos = jnp.cos(twist)
    twist_sin = jnp.sin(twist)
    turned_re = section_re * twist_cos + section_im * twist_sin
    turned_im = section_im * twist_cos - section_re * twist_sin
    freq_two = jnp.arange(PH, dtype=jnp.int32)
    theta_two = angle_table(second_index[:, None], freq_two[None, :], PB)
    cos_two = jnp.cos(theta_two)
    sin_two = jnp.sin(theta_two)
    spec_re = jnp.einsum("rbk,bm->rkm", turned_re, cos_two, precision=highest) + jnp.einsum(
        "rbk,bm->rkm", turned_im, sin_two, precision=highest
    )
    spec_im = jnp.einsum("rbk,bm->rkm", turned_im, cos_two, precision=highest) - jnp.einsum(
        "rbk,bm->rkm", turned_re, sin_two, precision=highest
    )
    scale = (2.0 / L) ** 0.5
    stacked = jnp.stack([spec_re, spec_im]) * scale
    span = PA // bands
    stacked = stacked.reshape(2, rows, span, bands, PH).transpose(3, 1, 0, 4, 2)
    return stacked.reshape(bands, rows, 2, PH * span)


def inverse_rows(spectra, band_ids, bands):
    count = spectra.shape[0]
    rows = spectra.shape[1]
    span = PA // bands
    parts = spectra.reshape(count, rows, 2, PH, span)
    part_re = parts[:, :, 0]
    part_im = parts[:, :, 1]
    freq_two = jnp.arange(PH, dtype=jnp.int32)
    second_index = jnp.arange(PB, dtype=jnp.int32)
    theta_two = angle_table(freq_two[:, None], second_index[None, :], PB)
    cos_two = jnp.cos(theta_two)
    sin_two = jnp.sin(theta_two)
    middle_re = jnp.einsum("brms,mn->brsn", part_re, cos_two, precision=highest) - jnp.einsum(
        "brms,mn->brsn", part_im, sin_two, precision=highest
    )
    middle_im = jnp.einsum("brms,mn->brsn", part_im, cos_two, precision=highest) + jnp.einsum(
        "brms,mn->brsn", part_re, sin_two, precision=highest
    )
    freq_one = jnp.arange(span, dtype=jnp.int32)[None, :] * bands + band_ids[:, None]
    twist = angle_table(freq_one[:, :, None], second_index[None, None, :], L)
    twist_cos = jnp.cos(twist)[:, None]
    twist_sin = jnp.sin(twist)[:, None]
    turned_re = middle_re * twist_cos - middle_im * twist_sin
    turned_im = middle_re * twist_sin + middle_im * twist_cos
    first_index = jnp.arange(PA, dtype=jnp.int32)
    theta_one = angle_table(freq_one[:, :, None], first_index[None, None, :], PA)
    grid = jnp.einsum(
        "brsn,bsa->ran", turned_re, jnp.cos(theta_one), precision=highest
    ) - jnp.einsum("brsn,bsa->ran", turned_im, jnp.sin(theta_one), precision=highest)
    return grid * (2.0 / L) ** 0.5


LANE = 128
SHIFTS = 8
CHUNK = 64


def stokes_body(k_ref, w_ref, o_ref, sh_ref):
    span = sh_ref.shape[1]
    total = w_ref.shape[1]
    steps = total // SHIFTS
    for s in range(SHIFTS):
        sh_ref[s] = k_ref[pl.ds(s, span), :]
    for part in range(total // CHUNK):

        def step(a, carry):
            acc_re, acc_im = carry
            base = pl.multiple_of(a * SHIFTS, SHIFTS)
            w_re = w_ref[0, pl.ds(base, SHIFTS), :]
            w_im = w_ref[1, pl.ds(base, SHIFTS), :]
            start = pl.multiple_of(part * CHUNK + total - SHIFTS - base, SHIFTS)
            for r in range(SHIFTS):
                slab = sh_ref[SHIFTS - 1 - r, pl.ds(start, CHUNK), :]
                acc_re = acc_re + slab * w_re[r : r + 1, :]
                acc_im = acc_im + slab * w_im[r : r + 1, :]
            return acc_re, acc_im

        zero = jnp.zeros((CHUNK, LANE), jnp.float32)
        acc_re, acc_im = lax.fori_loop(0, steps, step, (zero, zero))
        o_ref[0, part * CHUNK : (part + 1) * CHUNK, :] = acc_re
        o_ref[1, part * CHUNK : (part + 1) * CHUNK, :] = acc_im


def toeplitz_stokes(kernel_cols, weighted):
    taps, width = kernel_cols.shape
    total = weighted.shape[0]
    span = 2 * total
    flipped = jnp.pad(
        kernel_cols[::-1].astype(jnp.float32), ((0, span + SHIFTS - taps), (0, LANE - width))
    )
    source = jnp.pad(weighted.astype(jnp.float32).transpose(1, 0, 2), ((0, 0), (0, 0), (0, LANE - width)))
    out = pl.pallas_call(
        stokes_body,
        out_shape=jax.ShapeDtypeStruct((2, total, LANE), jnp.float32),
        scratch_shapes=[pltpu.VMEM((SHIFTS, span, LANE), jnp.float32)],
    )(flipped, source)
    return out[:, :, :width]


def per_device(gravity, coef, legendre, order_table, band_rows, kernel):
    bands = lax.axis_size("freq")
    blocks = lax.axis_size("lat")
    band_self = lax.axis_index("freq")
    block_self = lax.axis_index("lat")
    everyone = ("lat", "freq")
    devices = bands * blocks
    rows = gravity.shape[0]
    total_rows = rows * blocks
    mine = rows // bands
    band_width = kernel.shape[1]
    per_slot = coef.shape[0]
    held = blocks * per_slot
    sub = -(-band_width // blocks)
    share = sub - per_slot
    padded = held + share * blocks
    positions = order_table.reshape(blocks, bands, per_slot).transpose(1, 0, 2).reshape(bands, held) // bands
    selector = (
        positions[:, None, :] == jnp.arange(held, dtype=jnp.int32)[None, :, None]
    ).astype(jnp.float32)

    whole_rows = lax.all_to_all(gravity, "freq", split_axis=0, concat_axis=1, tiled=True)
    terms = forward_bands(whole_rows.reshape(mine, PA, PB), 0, bands)
    own = jnp.einsum("brct,bts->brcs", terms[..., :held], selector, precision=highest)
    own = own.reshape(bands, mine, 2, blocks, per_slot)
    rest = jnp.pad(terms[..., held:], ((0, 0), (0, 0), (0, 0), (0, padded - band_width)))
    rest = rest.reshape(bands, mine, 2, blocks, share)
    my_rows = lax.dynamic_slice_in_dim(band_rows, band_self * mine, mine, 0)
    weight = jnp.cos((20.0 + my_rows.astype(jnp.float32) / 60.0) * (np.pi / 180.0))
    carried = jnp.broadcast_to(weight[None, :, None, None, None], (bands, mine, 2, blocks, 1))
    payload = jnp.concatenate([own, rest, carried], axis=4).transpose(3, 0, 1, 2, 4)
    payload = payload.reshape(devices, mine, 2, sub + 1)
    payload, coef, legendre = lax.optimization_barrier((payload, coef, legendre))
    observed = lax.all_to_all(payload, everyone, split_axis=0, concat_axis=0, tiled=True)
    observed = observed.reshape(total_rows, 2, sub + 1)
    weight_all = observed[:, 0, sub]
    observed = observed[:, :, :sub]

    synth = jnp.einsum("ocn,onq->ocq", coef, legendre, preferred_element_type=jnp.float32).astype(
        jnp.bfloat16
    )
    model = jnp.pad(synth.astype(jnp.float32).transpose(2, 1, 0), ((0, 0), (0, 0), (0, share)))
    weighted = ((observed - model) * weight_all[:, None, None]).astype(jnp.bfloat16)

    own_cols = lax.dynamic_slice_in_dim(positions[band_self], block_self * per_slot, per_slot, 0)
    kernel_own = jnp.take(kernel, own_cols, axis=1)
    kernel_rest = lax.dynamic_slice_in_dim(
        jnp.pad(kernel, ((0, 0), (0, padded - band_width))), held + block_self * share, share, 1
    )
    stokes = toeplitz_stokes(jnp.concatenate([kernel_own, kernel_rest], axis=1), weighted)
    stokes = stokes.reshape(2, devices, mine, sub).transpose(1, 2, 0, 3)
    by_source = lax.all_to_all(stokes, everyone, split_axis=0, concat_axis=0, tiled=True)
    by_source = by_source.reshape(blocks, bands, mine, 2, sub).transpose(1, 2, 3, 0, 4)
    slots_back = by_source[..., :per_slot].reshape(bands, mine, 2, held)
    slots_back = jnp.einsum("brcs,bts->brct", slots_back, selector, precision=highest)
    rest_back = by_source[..., per_slot:].reshape(bands, mine, 2, blocks * share)
    by_band = jnp.concatenate([slots_back, rest_back], axis=3)[..., :band_width]
    grid_rows = inverse_rows(by_band, jnp.arange(bands, dtype=jnp.int32), bands)
    geoid = lax.all_to_all(grid_rows.reshape(mine, L), "freq", split_axis=1, concat_axis=0, tiled=True)
    return geoid


def solution(mesh):
    return jax.shard_map(
        per_device,
        mesh=mesh,
        in_specs=(
            P("lat", "freq"),
            P(("lat", "freq"), None, None),
            P(("lat", "freq"), None, None),
            P(),
            P("lat"),
            P(None, "freq"),
        ),
        out_specs=P("lat", "freq"),
        check_vma=False,
    )
```

```python
import jax
import jax.numpy as jnp
import numpy as np
from jax import lax
from jax.sharding import PartitionSpec as P
from jax.experimental import pallas as pl
from jax.experimental.pallas import tpu as pltpu

L = 21600
PA = 144
PB = 150
PH = 75


highest = lax.Precision.HIGHEST


def angle_table(first, second, period):
    phase = first * second % period
    return phase.astype(jnp.float32) * (2.0 * np.pi / period)


def forward_bands(grid, bands):
    rows = grid.shape[0]
    first_index = jnp.arange(PA, dtype=jnp.int32)
    theta_one = angle_table(first_index[:, None], first_index[None, :], PA)
    stage_one = jnp.concatenate([jnp.cos(theta_one), -jnp.sin(theta_one)], axis=1)
    section = jnp.einsum("rab,ak->rbk", grid, stage_one, precision=highest)
    section_re = section[..., :PA]
    section_im = section[..., PA:]
    second_index = jnp.arange(PB, dtype=jnp.int32)
    twist = angle_table(second_index[:, None], first_index[None, :], L)
    twist_cos = jnp.cos(twist)
    twist_sin = jnp.sin(twist)
    turned = jnp.concatenate(
        [section_re * twist_cos + section_im * twist_sin, section_im * twist_cos - section_re * twist_sin],
        axis=1,
    )
    freq_two = jnp.arange(PH, dtype=jnp.int32)
    theta_two = angle_table(second_index[:, None], freq_two[None, :], PB)
    cos_two = jnp.cos(theta_two)
    sin_two = jnp.sin(theta_two)
    stage_two = jnp.concatenate(
        [jnp.concatenate([cos_two, -sin_two], axis=1), jnp.concatenate([sin_two, cos_two], axis=1)], axis=0
    )
    spec = jnp.einsum("rbk,bm->rkm", turned, stage_two, precision=highest)
    scale = (2.0 / L) ** 0.5
    stacked = spec.reshape(rows, PA, 2, PH).transpose(2, 0, 1, 3) * scale
    span = PA // bands
    stacked = stacked.reshape(2, rows, span, bands, PH).transpose(3, 1, 0, 4, 2)
    return stacked.reshape(bands, rows, 2, PH * span)


def inverse_rows(spectra, bands):
    rows = spectra.shape[1]
    span = PA // bands
    parts = spectra.reshape(bands, rows, 2 * PH, span)
    freq_two = jnp.arange(PH, dtype=jnp.int32)
    second_index = jnp.arange(PB, dtype=jnp.int32)
    theta_two = angle_table(freq_two[:, None], second_index[None, :], PB)
    cos_two = jnp.cos(theta_two)
    sin_two = jnp.sin(theta_two)
    stage_two = jnp.concatenate(
        [jnp.concatenate([cos_two, sin_two], axis=1), jnp.concatenate([-sin_two, cos_two], axis=1)], axis=0
    )
    middle = jnp.einsum("brms,mn->brsn", parts, stage_two, precision=highest)
    middle_re = middle[..., :PB]
    middle_im = middle[..., PB:]
    band_ids = jnp.arange(bands, dtype=jnp.int32)
    freq_one = jnp.arange(span, dtype=jnp.int32)[None, :] * bands + band_ids[:, None]
    twist = angle_table(freq_one[:, :, None], second_index[None, None, :], L)
    twist_cos = jnp.cos(twist)[:, None]
    twist_sin = jnp.sin(twist)[:, None]
    turned = jnp.stack(
        [middle_re * twist_cos - middle_im * twist_sin, middle_re * twist_sin + middle_im * twist_cos]
    )
    first_index = jnp.arange(PA, dtype=jnp.int32)
    theta_one = angle_table(freq_one[:, :, None], first_index[None, None, :], PA)
    stage_one = jnp.stack([jnp.cos(theta_one), -jnp.sin(theta_one)])
    grid = jnp.einsum("pbrsn,pbsa->ran", turned, stage_one, precision=highest)
    return grid * (2.0 / L) ** 0.5


LANE = 128
SHIFTS = 8
CHUNK = 64


def stokes_body(k_ref, w_ref, o_ref, sh_ref):
    span = sh_ref.shape[1]
    total = w_ref.shape[1]
    steps = total // SHIFTS
    for s in range(SHIFTS):
        sh_ref[s] = k_ref[pl.ds(s, span), :]
    for part in range(total // CHUNK):

        def step(a, carry):
            acc_re, acc_im = carry
            base = pl.multiple_of(a * SHIFTS, SHIFTS)
            w_re = w_ref[0, pl.ds(base, SHIFTS), :]
            w_im = w_ref[1, pl.ds(base, SHIFTS), :]
            start = pl.multiple_of(part * CHUNK + total - SHIFTS - base, SHIFTS)
            for r in range(SHIFTS):
                slab = sh_ref[SHIFTS - 1 - r, pl.ds(start, CHUNK), :]
                acc_re = acc_re + slab * w_re[r : r + 1, :]
                acc_im = acc_im + slab * w_im[r : r + 1, :]
            return acc_re, acc_im

        zero = jnp.zeros((CHUNK, LANE), jnp.float32)
        acc_re, acc_im = lax.fori_loop(0, steps, step, (zero, zero))
        o_ref[0, part * CHUNK : (part + 1) * CHUNK, :] = acc_re
        o_ref[1, part * CHUNK : (part + 1) * CHUNK, :] = acc_im


def toeplitz_stokes(kernel_cols, weighted):
    taps, width = kernel_cols.shape
    total = weighted.shape[0]
    span = 2 * total
    flipped = jnp.pad(
        kernel_cols[::-1].astype(jnp.float32), ((0, span + SHIFTS - taps), (0, LANE - width))
    )
    source = jnp.pad(weighted.astype(jnp.float32).transpose(1, 0, 2), ((0, 0), (0, 0), (0, LANE - width)))
    out = pl.pallas_call(
        stokes_body,
        out_shape=jax.ShapeDtypeStruct((2, total, LANE), jnp.float32),
        scratch_shapes=[pltpu.VMEM((SHIFTS, span, LANE), jnp.float32)],
    )(flipped, source)
    return out[:, :, :width]


def per_device(gravity, coef, legendre, order_table, band_rows, kernel):
    bands = lax.axis_size("freq")
    blocks = lax.axis_size("lat")
    band_self = lax.axis_index("freq")
    block_self = lax.axis_index("lat")
    everyone = ("lat", "freq")
    devices = bands * blocks
    rows = gravity.shape[0]
    total_rows = rows * blocks
    mine = rows // bands
    band_width = kernel.shape[1]
    per_slot = coef.shape[0]
    held = blocks * per_slot
    sub = -(-band_width // blocks)
    share = sub - per_slot
    padded = held + share * blocks
    positions = order_table.reshape(blocks, bands, per_slot).transpose(1, 0, 2).reshape(bands, held) // bands
    selector = (
        positions[:, None, :] == jnp.arange(held, dtype=jnp.int32)[None, :, None]
    ).astype(jnp.float32)

    whole_rows = lax.all_to_all(gravity, "freq", split_axis=0, concat_axis=1, tiled=True)
    terms = forward_bands(whole_rows.reshape(mine, PA, PB), bands)
    own = jnp.einsum("brct,bts->brcs", terms[..., :held], selector, precision=highest)
    own = own.reshape(bands, mine, 2, blocks, per_slot)
    rest = jnp.pad(terms[..., held:], ((0, 0), (0, 0), (0, 0), (0, padded - band_width)))
    rest = rest.reshape(bands, mine, 2, blocks, share)
    my_rows = lax.dynamic_slice_in_dim(band_rows, band_self * mine, mine, 0)
    weight = jnp.cos((20.0 + my_rows.astype(jnp.float32) / 60.0) * (np.pi / 180.0))
    carried = jnp.broadcast_to(weight[None, :, None, None, None], (bands, mine, 2, blocks, 1))
    payload = jnp.concatenate([own, rest, carried], axis=4).transpose(3, 0, 1, 2, 4)
    payload = payload.reshape(devices, mine, 2, sub + 1)
    payload, coef, legendre = lax.optimization_barrier((payload, coef, legendre))
    observed = lax.all_to_all(payload, everyone, split_axis=0, concat_axis=0, tiled=True)
    observed = observed.reshape(total_rows, 2, sub + 1)
    weight_all = observed[:, 0, sub]
    observed = observed[:, :, :sub]

    synth = jnp.einsum("ocn,onq->ocq", coef, legendre, preferred_element_type=jnp.float32).astype(
        jnp.bfloat16
    )
    model = jnp.pad(synth.astype(jnp.float32).transpose(2, 1, 0), ((0, 0), (0, 0), (0, share)))
    weighted = ((observed - model) * weight_all[:, None, None]).astype(jnp.bfloat16)

    own_cols = lax.dynamic_slice_in_dim(positions[band_self], block_self * per_slot, per_slot, 0)
    kernel_own = jnp.take(kernel, own_cols, axis=1)
    kernel_rest = lax.dynamic_slice_in_dim(
        jnp.pad(kernel, ((0, 0), (0, padded - band_width))), held + block_self * share, share, 1
    )
    stokes = toeplitz_stokes(jnp.concatenate([kernel_own, kernel_rest], axis=1), weighted)
    stokes = stokes.reshape(2, devices, mine, sub).transpose(1, 2, 0, 3)
    by_source = lax.all_to_all(stokes, everyone, split_axis=0, concat_axis=0, tiled=True)
    by_source = by_source.reshape(blocks, bands, mine, 2, sub).transpose(1, 2, 3, 0, 4)
    slots_back = by_source[..., :per_slot].reshape(bands, mine, 2, held)
    slots_back = jnp.einsum("brcs,bts->brct", slots_back, selector, precision=highest)
    rest_back = by_source[..., per_slot:].reshape(bands, mine, 2, blocks * share)
    by_band = jnp.concatenate([slots_back, rest_back], axis=3)[..., :band_width]
    grid_rows = inverse_rows(by_band, bands)
    geoid = lax.all_to_all(grid_rows.reshape(mine, L), "freq", split_axis=1, concat_axis=0, tiled=True)
    return geoid


def solution(mesh):
    return jax.shard_map(
        per_device,
        mesh=mesh,
        in_specs=(
            P("lat", "freq"),
            P(("lat", "freq"), None, None),
            P(("lat", "freq"), None, None),
            P(),
            P("lat"),
            P(None, "freq"),
        ),
        out_specs=P("lat", "freq"),
        check_vma=False,
    )
```

```python
import jax
import jax.numpy as jnp
import numpy as np
from jax import lax
from jax.sharding import PartitionSpec as P
from jax.experimental import pallas as pl
from jax.experimental.pallas import tpu as pltpu

L = 21600
PA = 144
PB = 150
PH = 75


highest = lax.Precision.HIGHEST


def angle_table(first, second, period):
    phase = (first * second) % period
    return phase.astype(np.float64) * (2.0 * np.pi / period)


def constant(values):
    return jnp.asarray(np.asarray(values, dtype=np.float32))


def forward_bands(grid, bands):
    rows = grid.shape[0]
    first_index = np.arange(PA)
    theta_one = angle_table(first_index[:, None], first_index[None, :], PA)
    stage_one = constant(np.concatenate([np.cos(theta_one), -np.sin(theta_one)], axis=1))
    section = jnp.einsum("rab,ak->rbk", grid, stage_one, precision=highest)
    section_re = section[..., :PA]
    section_im = section[..., PA:]
    second_index = np.arange(PB)
    twist = angle_table(second_index[:, None], first_index[None, :], L)
    twist_cos = constant(np.cos(twist))
    twist_sin = constant(np.sin(twist))
    turned = jnp.concatenate(
        [section_re * twist_cos + section_im * twist_sin, section_im * twist_cos - section_re * twist_sin],
        axis=1,
    )
    freq_two = np.arange(PH)
    theta_two = angle_table(second_index[:, None], freq_two[None, :], PB)
    cos_two = np.cos(theta_two)
    sin_two = np.sin(theta_two)
    stage_two = constant(
        np.concatenate([np.concatenate([cos_two, -sin_two], axis=1), np.concatenate([sin_two, cos_two], axis=1)])
    )
    spec = jnp.einsum("rbk,bm->rkm", turned, stage_two, precision=highest)
    scale = (2.0 / L) ** 0.5
    stacked = spec.reshape(rows, PA, 2, PH).transpose(2, 0, 1, 3) * scale
    span = PA // bands
    stacked = stacked.reshape(2, rows, span, bands, PH).transpose(3, 1, 0, 4, 2)
    return stacked.reshape(bands, rows, 2, PH * span)


def inverse_rows(spectra, bands):
    rows = spectra.shape[1]
    span = PA // bands
    parts = spectra.reshape(bands, rows, 2 * PH, span)
    freq_two = np.arange(PH)
    second_index = np.arange(PB)
    theta_two = angle_table(freq_two[:, None], second_index[None, :], PB)
    cos_two = np.cos(theta_two)
    sin_two = np.sin(theta_two)
    stage_two = constant(
        np.concatenate([np.concatenate([cos_two, sin_two], axis=1), np.concatenate([-sin_two, cos_two], axis=1)])
    )
    middle = jnp.einsum("brms,mn->brsn", parts, stage_two, precision=highest)
    middle_re = middle[..., :PB]
    middle_im = middle[..., PB:]
    band_ids = np.arange(bands)
    freq_one = np.arange(span)[None, :] * bands + band_ids[:, None]
    twist = angle_table(freq_one[:, :, None], second_index[None, None, :], L)
    twist_cos = constant(np.cos(twist))[:, None]
    twist_sin = constant(np.sin(twist))[:, None]
    turned = jnp.stack(
        [middle_re * twist_cos - middle_im * twist_sin, middle_re * twist_sin + middle_im * twist_cos]
    )
    first_index = np.arange(PA)
    theta_one = angle_table(freq_one[:, :, None], first_index[None, None, :], PA)
    stage_one = constant(np.stack([np.cos(theta_one), -np.sin(theta_one)]))
    grid = jnp.einsum("pbrsn,pbsa->ran", turned, stage_one, precision=highest)
    return grid * (2.0 / L) ** 0.5


LANE = 128
SHIFTS = 8
CHUNK = 64


def stokes_body(k_ref, w_ref, o_ref, sh_ref):
    span = sh_ref.shape[1]
    total = w_ref.shape[1]
    steps = total // SHIFTS
    for s in range(SHIFTS):
        sh_ref[s] = k_ref[pl.ds(s, span), :]
    for part in range(total // CHUNK):

        def step(a, carry):
            acc_re, acc_im = carry
            base = pl.multiple_of(a * SHIFTS, SHIFTS)
            w_re = w_ref[0, pl.ds(base, SHIFTS), :]
            w_im = w_ref[1, pl.ds(base, SHIFTS), :]
            start = pl.multiple_of(part * CHUNK + total - SHIFTS - base, SHIFTS)
            for r in range(SHIFTS):
                slab = sh_ref[SHIFTS - 1 - r, pl.ds(start, CHUNK), :]
                acc_re = acc_re + slab * w_re[r : r + 1, :]
                acc_im = acc_im + slab * w_im[r : r + 1, :]
            return acc_re, acc_im

        zero = jnp.zeros((CHUNK, LANE), jnp.float32)
        acc_re, acc_im = lax.fori_loop(0, steps, step, (zero, zero))
        o_ref[0, part * CHUNK : (part + 1) * CHUNK, :] = acc_re
        o_ref[1, part * CHUNK : (part + 1) * CHUNK, :] = acc_im


def toeplitz_stokes(kernel_cols, weighted):
    taps, width = kernel_cols.shape
    total = weighted.shape[0]
    span = 2 * total
    flipped = jnp.pad(
        kernel_cols[::-1].astype(jnp.float32), ((0, span + SHIFTS - taps), (0, LANE - width))
    )
    source = jnp.pad(weighted.astype(jnp.float32).transpose(1, 0, 2), ((0, 0), (0, 0), (0, LANE - width)))
    out = pl.pallas_call(
        stokes_body,
        out_shape=jax.ShapeDtypeStruct((2, total, LANE), jnp.float32),
        scratch_shapes=[pltpu.VMEM((SHIFTS, span, LANE), jnp.float32)],
    )(flipped, source)
    return out[:, :, :width]


def per_device(gravity, coef, legendre, order_table, band_rows, kernel):
    bands = lax.axis_size("freq")
    blocks = lax.axis_size("lat")
    band_self = lax.axis_index("freq")
    block_self = lax.axis_index("lat")
    everyone = ("lat", "freq")
    devices = bands * blocks
    rows = gravity.shape[0]
    total_rows = rows * blocks
    mine = rows // bands
    band_width = kernel.shape[1]
    per_slot = coef.shape[0]
    held = blocks * per_slot
    sub = -(-band_width // blocks)
    share = sub - per_slot
    padded = held + share * blocks
    positions = order_table.reshape(blocks, bands, per_slot).transpose(1, 0, 2).reshape(bands, held) // bands
    selector = (
        positions[:, None, :] == jnp.arange(held, dtype=jnp.int32)[None, :, None]
    ).astype(jnp.float32)

    whole_rows = lax.all_to_all(gravity, "freq", split_axis=0, concat_axis=1, tiled=True)
    terms = forward_bands(whole_rows.reshape(mine, PA, PB), bands)
    own = jnp.einsum("brct,bts->brcs", terms[..., :held], selector, precision=highest)
    own = own.reshape(bands, mine, 2, blocks, per_slot)
    rest = jnp.pad(terms[..., held:], ((0, 0), (0, 0), (0, 0), (0, padded - band_width)))
    rest = rest.reshape(bands, mine, 2, blocks, share)
    my_rows = lax.dynamic_slice_in_dim(band_rows, band_self * mine, mine, 0)
    weight = jnp.cos((20.0 + my_rows.astype(jnp.float32) / 60.0) * (np.pi / 180.0))
    carried = jnp.broadcast_to(weight[None, :, None, None, None], (bands, mine, 2, blocks, 1))
    payload = jnp.concatenate([own, rest, carried], axis=4).transpose(3, 0, 1, 2, 4)
    payload = payload.reshape(devices, mine, 2, sub + 1)
    payload, coef, legendre = lax.optimization_barrier((payload, coef, legendre))
    observed = lax.all_to_all(payload, everyone, split_axis=0, concat_axis=0, tiled=True)
    observed = observed.reshape(total_rows, 2, sub + 1)
    weight_all = observed[:, 0, sub]
    observed = observed[:, :, :sub]

    synth = jnp.einsum("ocn,onq->ocq", coef, legendre, preferred_element_type=jnp.float32).astype(
        jnp.bfloat16
    )
    model = jnp.pad(synth.astype(jnp.float32).transpose(2, 1, 0), ((0, 0), (0, 0), (0, share)))
    weighted = ((observed - model) * weight_all[:, None, None]).astype(jnp.bfloat16)

    own_cols = lax.dynamic_slice_in_dim(positions[band_self], block_self * per_slot, per_slot, 0)
    kernel_own = jnp.take(kernel, own_cols, axis=1)
    kernel_rest = lax.dynamic_slice_in_dim(
        jnp.pad(kernel, ((0, 0), (0, padded - band_width))), held + block_self * share, share, 1
    )
    stokes = toeplitz_stokes(jnp.concatenate([kernel_own, kernel_rest], axis=1), weighted)
    stokes = stokes.reshape(2, devices, mine, sub).transpose(1, 2, 0, 3)
    by_source = lax.all_to_all(stokes, everyone, split_axis=0, concat_axis=0, tiled=True)
    by_source = by_source.reshape(blocks, bands, mine, 2, sub).transpose(1, 2, 3, 0, 4)
    slots_back = by_source[..., :per_slot].reshape(bands, mine, 2, held)
    slots_back = jnp.einsum("brcs,bts->brct", slots_back, selector, precision=highest)
    rest_back = by_source[..., per_slot:].reshape(bands, mine, 2, blocks * share)
    by_band = jnp.concatenate([slots_back, rest_back], axis=3)[..., :band_width]
    grid_rows = inverse_rows(by_band, bands)
    geoid = lax.all_to_all(grid_rows.reshape(mine, L), "freq", split_axis=1, concat_axis=0, tiled=True)
    return geoid


def solution(mesh):
    return jax.shard_map(
        per_device,
        mesh=mesh,
        in_specs=(
            P("lat", "freq"),
            P(("lat", "freq"), None, None),
            P(("lat", "freq"), None, None),
            P(),
            P("lat"),
            P(None, "freq"),
        ),
        out_specs=P("lat", "freq"),
        check_vma=False,
    )
```

```python
import jax
import jax.numpy as jnp
import numpy as np
from jax import lax
from jax.sharding import PartitionSpec as P
from jax.experimental import pallas as pl
from jax.experimental.pallas import tpu as pltpu

L = 21600
PA = 144
PB = 150
PH = 75


precise = lax.Precision.HIGH


def angle_table(first, second, period):
    phase = (first * second) % period
    return phase.astype(np.float64) * (2.0 * np.pi / period)


def constant(values):
    return jnp.asarray(np.asarray(values, dtype=np.float32))


def forward_bands(grid, bands):
    rows = grid.shape[0]
    first_index = np.arange(PA)
    theta_one = angle_table(first_index[:, None], first_index[None, :], PA)
    stage_one = constant(np.concatenate([np.cos(theta_one), -np.sin(theta_one)], axis=1))
    section = jnp.einsum("rab,ak->rbk", grid, stage_one, precision=precise)
    section_re = section[..., :PA]
    section_im = section[..., PA:]
    second_index = np.arange(PB)
    twist = angle_table(second_index[:, None], first_index[None, :], L)
    twist_cos = constant(np.cos(twist))
    twist_sin = constant(np.sin(twist))
    turned = jnp.concatenate(
        [section_re * twist_cos + section_im * twist_sin, section_im * twist_cos - section_re * twist_sin],
        axis=1,
    )
    freq_two = np.arange(PH)
    theta_two = angle_table(second_index[:, None], freq_two[None, :], PB)
    cos_two = np.cos(theta_two)
    sin_two = np.sin(theta_two)
    stage_two = constant(
        np.concatenate([np.concatenate([cos_two, -sin_two], axis=1), np.concatenate([sin_two, cos_two], axis=1)])
    )
    spec = jnp.einsum("rbk,bm->rkm", turned, stage_two, precision=precise)
    scale = (2.0 / L) ** 0.5
    stacked = spec.reshape(rows, PA, 2, PH).transpose(2, 0, 1, 3) * scale
    span = PA // bands
    stacked = stacked.reshape(2, rows, span, bands, PH).transpose(3, 1, 0, 4, 2)
    return stacked.reshape(bands, rows, 2, PH * span)


def inverse_rows(spectra, bands):
    rows = spectra.shape[1]
    span = PA // bands
    parts = spectra.reshape(bands, rows, 2 * PH, span)
    freq_two = np.arange(PH)
    second_index = np.arange(PB)
    theta_two = angle_table(freq_two[:, None], second_index[None, :], PB)
    cos_two = np.cos(theta_two)
    sin_two = np.sin(theta_two)
    stage_two = constant(
        np.concatenate([np.concatenate([cos_two, sin_two], axis=1), np.concatenate([-sin_two, cos_two], axis=1)])
    )
    middle = jnp.einsum("brms,mn->brsn", parts, stage_two, precision=precise)
    middle_re = middle[..., :PB]
    middle_im = middle[..., PB:]
    band_ids = np.arange(bands)
    freq_one = np.arange(span)[None, :] * bands + band_ids[:, None]
    twist = angle_table(freq_one[:, :, None], second_index[None, None, :], L)
    twist_cos = constant(np.cos(twist))[:, None]
    twist_sin = constant(np.sin(twist))[:, None]
    turned = jnp.stack(
        [middle_re * twist_cos - middle_im * twist_sin, middle_re * twist_sin + middle_im * twist_cos]
    )
    first_index = np.arange(PA)
    theta_one = angle_table(freq_one[:, :, None], first_index[None, None, :], PA)
    stage_one = constant(np.stack([np.cos(theta_one), -np.sin(theta_one)]))
    grid = jnp.einsum("pbrsn,pbsa->ran", turned, stage_one, precision=precise)
    return grid * (2.0 / L) ** 0.5


LANE = 128
SHIFTS = 8
CHUNK = 64


def stokes_body(k_ref, w_ref, o_ref, sh_ref):
    span = sh_ref.shape[1]
    total = w_ref.shape[1]
    steps = total // SHIFTS
    for s in range(SHIFTS):
        sh_ref[s] = k_ref[pl.ds(s, span), :]
    for part in range(total // CHUNK):

        def step(a, carry):
            acc_re, acc_im = carry
            base = pl.multiple_of(a * SHIFTS, SHIFTS)
            w_re = w_ref[0, pl.ds(base, SHIFTS), :]
            w_im = w_ref[1, pl.ds(base, SHIFTS), :]
            start = pl.multiple_of(part * CHUNK + total - SHIFTS - base, SHIFTS)
            for r in range(SHIFTS):
                slab = sh_ref[SHIFTS - 1 - r, pl.ds(start, CHUNK), :]
                acc_re = acc_re + slab * w_re[r : r + 1, :]
                acc_im = acc_im + slab * w_im[r : r + 1, :]
            return acc_re, acc_im

        zero = jnp.zeros((CHUNK, LANE), jnp.float32)
        acc_re, acc_im = lax.fori_loop(0, steps, step, (zero, zero))
        o_ref[0, part * CHUNK : (part + 1) * CHUNK, :] = acc_re
        o_ref[1, part * CHUNK : (part + 1) * CHUNK, :] = acc_im


def toeplitz_stokes(kernel_cols, weighted):
    taps, width = kernel_cols.shape
    total = weighted.shape[0]
    span = 2 * total
    flipped = jnp.pad(
        kernel_cols[::-1].astype(jnp.float32), ((0, span + SHIFTS - taps), (0, LANE - width))
    )
    source = jnp.pad(weighted.astype(jnp.float32).transpose(1, 0, 2), ((0, 0), (0, 0), (0, LANE - width)))
    out = pl.pallas_call(
        stokes_body,
        out_shape=jax.ShapeDtypeStruct((2, total, LANE), jnp.float32),
        scratch_shapes=[pltpu.VMEM((SHIFTS, span, LANE), jnp.float32)],
    )(flipped, source)
    return out[:, :, :width]


def per_device(gravity, coef, legendre, order_table, band_rows, kernel):
    bands = lax.axis_size("freq")
    blocks = lax.axis_size("lat")
    band_self = lax.axis_index("freq")
    block_self = lax.axis_index("lat")
    everyone = ("lat", "freq")
    devices = bands * blocks
    rows = gravity.shape[0]
    total_rows = rows * blocks
    mine = rows // bands
    band_width = kernel.shape[1]
    per_slot = coef.shape[0]
    held = blocks * per_slot
    sub = -(-band_width // blocks)
    share = sub - per_slot
    padded = held + share * blocks
    positions = order_table.reshape(blocks, bands, per_slot).transpose(1, 0, 2).reshape(bands, held) // bands
    selector = (
        positions[:, None, :] == jnp.arange(held, dtype=jnp.int32)[None, :, None]
    ).astype(jnp.float32)

    whole_rows = lax.all_to_all(gravity, "freq", split_axis=0, concat_axis=1, tiled=True)
    terms = forward_bands(whole_rows.reshape(mine, PA, PB), bands)
    own = jnp.einsum("brct,bts->brcs", terms[..., :held], selector, precision=precise)
    own = own.reshape(bands, mine, 2, blocks, per_slot)
    rest = jnp.pad(terms[..., held:], ((0, 0), (0, 0), (0, 0), (0, padded - band_width)))
    rest = rest.reshape(bands, mine, 2, blocks, share)
    my_rows = lax.dynamic_slice_in_dim(band_rows, band_self * mine, mine, 0)
    weight = jnp.cos((20.0 + my_rows.astype(jnp.float32) / 60.0) * (np.pi / 180.0))
    carried = jnp.broadcast_to(weight[None, :, None, None, None], (bands, mine, 2, blocks, 1))
    payload = jnp.concatenate([own, rest, carried], axis=4).transpose(3, 0, 1, 2, 4)
    payload = payload.reshape(devices, mine, 2, sub + 1)
    payload, coef, legendre = lax.optimization_barrier((payload, coef, legendre))
    observed = lax.all_to_all(payload, everyone, split_axis=0, concat_axis=0, tiled=True)
    observed = observed.reshape(total_rows, 2, sub + 1)
    weight_all = observed[:, 0, sub]
    observed = observed[:, :, :sub]

    synth = jnp.einsum("ocn,onq->ocq", coef, legendre, preferred_element_type=jnp.float32).astype(
        jnp.bfloat16
    )
    model = jnp.pad(synth.astype(jnp.float32).transpose(2, 1, 0), ((0, 0), (0, 0), (0, share)))
    weighted = ((observed - model) * weight_all[:, None, None]).astype(jnp.bfloat16)

    own_cols = lax.dynamic_slice_in_dim(positions[band_self], block_self * per_slot, per_slot, 0)
    kernel_own = jnp.take(kernel, own_cols, axis=1)
    kernel_rest = lax.dynamic_slice_in_dim(
        jnp.pad(kernel, ((0, 0), (0, padded - band_width))), held + block_self * share, share, 1
    )
    stokes = toeplitz_stokes(jnp.concatenate([kernel_own, kernel_rest], axis=1), weighted)
    stokes = stokes.reshape(2, devices, mine, sub).transpose(1, 2, 0, 3)
    by_source = lax.all_to_all(stokes, everyone, split_axis=0, concat_axis=0, tiled=True)
    by_source = by_source.reshape(blocks, bands, mine, 2, sub).transpose(1, 2, 3, 0, 4)
    slots_back = by_source[..., :per_slot].reshape(bands, mine, 2, held)
    slots_back = jnp.einsum("brcs,bts->brct", slots_back, selector, precision=precise)
    rest_back = by_source[..., per_slot:].reshape(bands, mine, 2, blocks * share)
    by_band = jnp.concatenate([slots_back, rest_back], axis=3)[..., :band_width]
    grid_rows = inverse_rows(by_band, bands)
    geoid = lax.all_to_all(grid_rows.reshape(mine, L), "freq", split_axis=1, concat_axis=0, tiled=True)
    return geoid


def solution(mesh):
    return jax.shard_map(
        per_device,
        mesh=mesh,
        in_specs=(
            P("lat", "freq"),
            P(("lat", "freq"), None, None),
            P(("lat", "freq"), None, None),
            P(),
            P("lat"),
            P(None, "freq"),
        ),
        out_specs=P("lat", "freq"),
        check_vma=False,
    )
```

```python
import jax
import jax.numpy as jnp
import numpy as np
from jax import lax
from jax.sharding import PartitionSpec as P
from jax.experimental import pallas as pl
from jax.experimental.pallas import tpu as pltpu

L = 21600
PA = 144
PB = 150
PH = 75


precise = lax.Precision.HIGH


def angle_table(first, second, period):
    phase = (first * second) % period
    return phase.astype(np.float64) * (2.0 * np.pi / period)


def constant(values):
    return jnp.asarray(np.asarray(values, dtype=np.float32))


def forward_bands(grid, bands):
    rows = grid.shape[0]
    first_index = np.arange(PA)
    theta_one = angle_table(first_index[:, None], first_index[None, :], PA)
    stage_one = constant(np.concatenate([np.cos(theta_one), -np.sin(theta_one)], axis=1))
    section = jnp.einsum("rab,ak->rbk", grid, stage_one, precision=precise)
    section_re = section[..., :PA]
    section_im = section[..., PA:]
    second_index = np.arange(PB)
    twist = angle_table(second_index[:, None], first_index[None, :], L)
    twist_cos = constant(np.cos(twist))
    twist_sin = constant(np.sin(twist))
    turned = jnp.concatenate(
        [section_re * twist_cos + section_im * twist_sin, section_im * twist_cos - section_re * twist_sin],
        axis=1,
    )
    freq_two = np.arange(PH)
    theta_two = angle_table(second_index[:, None], freq_two[None, :], PB)
    cos_two = np.cos(theta_two)
    sin_two = np.sin(theta_two)
    stage_two = constant(
        np.concatenate([np.concatenate([cos_two, -sin_two], axis=1), np.concatenate([sin_two, cos_two], axis=1)])
    )
    spec = jnp.einsum("rbk,bm->rkm", turned, stage_two, precision=precise)
    scale = (2.0 / L) ** 0.5
    stacked = spec.reshape(rows, PA, 2, PH).transpose(2, 0, 1, 3) * scale
    span = PA // bands
    stacked = stacked.reshape(2, rows, span, bands, PH).transpose(3, 1, 0, 4, 2)
    return stacked.reshape(bands, rows, 2, PH * span)


def inverse_rows(spectra, bands, band_self):
    rows = spectra.shape[1]
    span = PA // bands
    parts = spectra.reshape(bands, rows, 2 * PH, span)
    freq_two = np.arange(PH)
    second_index = np.arange(PB)
    theta_two = angle_table(freq_two[:, None], second_index[None, :], PB)
    cos_two = np.cos(theta_two)
    sin_two = np.sin(theta_two)
    stage_two = constant(
        np.concatenate([np.concatenate([cos_two, sin_two], axis=1), np.concatenate([-sin_two, cos_two], axis=1)])
    )
    middle = jnp.einsum("brms,mn->brsn", parts, stage_two, precision=precise)
    middle_re = middle[..., :PB]
    middle_im = middle[..., PB:]
    band_ids = np.arange(bands)
    freq_one = np.arange(span)[None, :] * bands + band_ids[:, None]
    twist = angle_table(freq_one[:, :, None], second_index[None, None, :], L)
    twist_cos = constant(np.cos(twist))[:, None]
    twist_sin = constant(np.sin(twist))[:, None]
    turned = jnp.stack(
        [middle_re * twist_cos - middle_im * twist_sin, middle_re * twist_sin + middle_im * twist_cos]
    )
    first_index = np.arange(PA)
    theta_one = angle_table(freq_one[:, :, None], first_index[None, None, :], PA)
    stage_one = constant(np.stack([np.cos(theta_one), -np.sin(theta_one)]))
    stage_one = lax.dynamic_slice_in_dim(stage_one, band_self * span, span, 3)
    grid = jnp.einsum("pbrsn,pbsa->ran", turned, stage_one, precision=precise)
    return grid * (2.0 / L) ** 0.5


LANE = 128
SHIFTS = 8
CHUNK = 64


def stokes_body(k_ref, w_ref, o_ref, sh_ref):
    span = sh_ref.shape[1]
    total = w_ref.shape[1]
    steps = total // SHIFTS
    for s in range(SHIFTS):
        sh_ref[s] = k_ref[pl.ds(s, span), :]
    for part in range(total // CHUNK):

        def step(a, carry):
            acc_re, acc_im = carry
            base = pl.multiple_of(a * SHIFTS, SHIFTS)
            w_re = w_ref[0, pl.ds(base, SHIFTS), :]
            w_im = w_ref[1, pl.ds(base, SHIFTS), :]
            start = pl.multiple_of(part * CHUNK + total - SHIFTS - base, SHIFTS)
            for r in range(SHIFTS):
                slab = sh_ref[SHIFTS - 1 - r, pl.ds(start, CHUNK), :]
                acc_re = acc_re + slab * w_re[r : r + 1, :]
                acc_im = acc_im + slab * w_im[r : r + 1, :]
            return acc_re, acc_im

        zero = jnp.zeros((CHUNK, LANE), jnp.float32)
        acc_re, acc_im = lax.fori_loop(0, steps, step, (zero, zero))
        o_ref[0, part * CHUNK : (part + 1) * CHUNK, :] = acc_re
        o_ref[1, part * CHUNK : (part + 1) * CHUNK, :] = acc_im


def toeplitz_stokes(kernel_cols, weighted):
    taps, width = kernel_cols.shape
    total = weighted.shape[0]
    span = 2 * total
    flipped = jnp.pad(
        kernel_cols[::-1].astype(jnp.float32), ((0, span + SHIFTS - taps), (0, LANE - width))
    )
    source = jnp.pad(weighted.astype(jnp.float32).transpose(1, 0, 2), ((0, 0), (0, 0), (0, LANE - width)))
    out = pl.pallas_call(
        stokes_body,
        out_shape=jax.ShapeDtypeStruct((2, total, LANE), jnp.float32),
        scratch_shapes=[pltpu.VMEM((SHIFTS, span, LANE), jnp.float32)],
    )(flipped, source)
    return out[:, :, :width]


def per_device(gravity, coef, legendre, order_table, band_rows, kernel):
    bands = lax.axis_size("freq")
    blocks = lax.axis_size("lat")
    band_self = lax.axis_index("freq")
    block_self = lax.axis_index("lat")
    everyone = ("lat", "freq")
    devices = bands * blocks
    rows = gravity.shape[0]
    total_rows = rows * blocks
    mine = rows // bands
    band_width = kernel.shape[1]
    per_slot = coef.shape[0]
    held = blocks * per_slot
    sub = -(-band_width // blocks)
    share = sub - per_slot
    padded = held + share * blocks
    positions = order_table.reshape(blocks, bands, per_slot).transpose(1, 0, 2).reshape(bands, held) // bands
    selector = (
        positions[:, None, :] == jnp.arange(held, dtype=jnp.int32)[None, :, None]
    ).astype(jnp.float32)

    whole_rows = lax.all_to_all(gravity, "freq", split_axis=0, concat_axis=1, tiled=True)
    terms = forward_bands(whole_rows.reshape(mine, PA, PB), bands)
    own = jnp.einsum("brct,bts->brcs", terms[..., :held], selector, precision=precise)
    own = own.reshape(bands, mine, 2, blocks, per_slot)
    rest = jnp.pad(terms[..., held:], ((0, 0), (0, 0), (0, 0), (0, padded - band_width)))
    rest = rest.reshape(bands, mine, 2, blocks, share)
    my_rows = lax.dynamic_slice_in_dim(band_rows, band_self * mine, mine, 0)
    weight = jnp.cos((20.0 + my_rows.astype(jnp.float32) / 60.0) * (np.pi / 180.0))
    carried = jnp.broadcast_to(weight[None, :, None, None, None], (bands, mine, 2, blocks, 1))
    payload = jnp.concatenate([own, rest, carried], axis=4).transpose(3, 0, 1, 2, 4)
    payload = payload.reshape(devices, mine, 2, sub + 1)
    payload, coef, legendre = lax.optimization_barrier((payload, coef, legendre))
    observed = lax.all_to_all(payload, everyone, split_axis=0, concat_axis=0, tiled=True)
    observed = observed.reshape(total_rows, 2, sub + 1)
    weight_all = observed[:, 0, sub]
    observed = observed[:, :, :sub]

    synth = jnp.einsum("ocn,onq->ocq", coef, legendre, preferred_element_type=jnp.float32).astype(
        jnp.bfloat16
    )
    model = jnp.pad(synth.astype(jnp.float32).transpose(2, 1, 0), ((0, 0), (0, 0), (0, share)))
    weighted = ((observed - model) * weight_all[:, None, None]).astype(jnp.bfloat16)

    own_cols = lax.dynamic_slice_in_dim(positions[band_self], block_self * per_slot, per_slot, 0)
    kernel_own = jnp.take(kernel, own_cols, axis=1)
    kernel_rest = lax.dynamic_slice_in_dim(
        jnp.pad(kernel, ((0, 0), (0, padded - band_width))), held + block_self * share, share, 1
    )
    stokes = toeplitz_stokes(jnp.concatenate([kernel_own, kernel_rest], axis=1), weighted)
    stokes = stokes.reshape(2, blocks, rows, sub).transpose(1, 2, 0, 3)
    stokes = jnp.broadcast_to(stokes[:, None], (blocks, bands, rows, 2, sub)).reshape(devices, rows, 2, sub)
    by_source = lax.all_to_all(stokes, everyone, split_axis=0, concat_axis=0, tiled=True)
    by_source = by_source.reshape(blocks, bands, rows, 2, sub).transpose(1, 2, 3, 0, 4)
    slots_back = by_source[..., :per_slot].reshape(bands, rows, 2, held)
    slots_back = jnp.einsum("brcs,bts->brct", slots_back, selector, precision=precise)
    rest_back = by_source[..., per_slot:].reshape(bands, rows, 2, blocks * share)
    by_band = jnp.concatenate([slots_back, rest_back], axis=3)[..., :band_width]
    grid_rows = inverse_rows(by_band, bands, band_self)
    geoid = grid_rows.reshape(rows, L // bands)
    return geoid


def solution(mesh):
    return jax.shard_map(
        per_device,
        mesh=mesh,
        in_specs=(
            P("lat", "freq"),
            P(("lat", "freq"), None, None),
            P(("lat", "freq"), None, None),
            P(),
            P("lat"),
            P(None, "freq"),
        ),
        out_specs=P("lat", "freq"),
        check_vma=False,
    )
```

```python
import jax
import jax.numpy as jnp
import numpy as np
from jax import lax
from jax.sharding import PartitionSpec as P
from jax.experimental import pallas as pl
from jax.experimental.pallas import tpu as pltpu

L = 21600
PA = 144
PB = 150
PH = 75


precise = lax.Precision.HIGH


def angle_table(first, second, period):
    phase = (first * second) % period
    return phase.astype(np.float64) * (2.0 * np.pi / period)


def constant(values):
    return jnp.asarray(np.asarray(values, dtype=np.float32))


def forward_bands(grid, bands):
    rows = grid.shape[0]
    first_index = np.arange(PA)
    theta_one = angle_table(first_index[:, None], first_index[None, :], PA)
    stage_one = constant(np.concatenate([np.cos(theta_one), -np.sin(theta_one)], axis=1))
    section = jnp.einsum("rab,ak->rbk", grid, stage_one, precision=precise)
    section_re = section[..., :PA]
    section_im = section[..., PA:]
    second_index = np.arange(PB)
    twist = angle_table(second_index[:, None], first_index[None, :], L)
    twist_cos = constant(np.cos(twist))
    twist_sin = constant(np.sin(twist))
    turned = jnp.concatenate(
        [section_re * twist_cos + section_im * twist_sin, section_im * twist_cos - section_re * twist_sin],
        axis=1,
    )
    freq_two = np.arange(PH)
    theta_two = angle_table(second_index[:, None], freq_two[None, :], PB)
    cos_two = np.cos(theta_two)
    sin_two = np.sin(theta_two)
    stage_two = constant(
        np.concatenate([np.concatenate([cos_two, -sin_two], axis=1), np.concatenate([sin_two, cos_two], axis=1)])
    )
    spec = jnp.einsum("rbk,bm->rkm", turned, stage_two, precision=precise)
    scale = (2.0 / L) ** 0.5
    stacked = spec.reshape(rows, PA, 2, PH).transpose(2, 0, 1, 3) * scale
    span = PA // bands
    stacked = stacked.reshape(2, rows, span, bands, PH).transpose(3, 1, 0, 4, 2)
    return stacked.reshape(bands, rows, 2, PH * span)


def inverse_rows(spectra, bands):
    rows = spectra.shape[1]
    span = PA // bands
    parts = spectra.reshape(bands, rows, 2 * PH, span)
    freq_two = np.arange(PH)
    second_index = np.arange(PB)
    theta_two = angle_table(freq_two[:, None], second_index[None, :], PB)
    cos_two = np.cos(theta_two)
    sin_two = np.sin(theta_two)
    stage_two = constant(
        np.concatenate([np.concatenate([cos_two, sin_two], axis=1), np.concatenate([-sin_two, cos_two], axis=1)])
    )
    middle = jnp.einsum("brms,mn->brsn", parts, stage_two, precision=precise)
    middle_re = middle[..., :PB]
    middle_im = middle[..., PB:]
    band_ids = np.arange(bands)
    freq_one = np.arange(span)[None, :] * bands + band_ids[:, None]
    twist = angle_table(freq_one[:, :, None], second_index[None, None, :], L)
    twist_cos = constant(np.cos(twist))[:, None]
    twist_sin = constant(np.sin(twist))[:, None]
    turned = jnp.stack(
        [middle_re * twist_cos - middle_im * twist_sin, middle_re * twist_sin + middle_im * twist_cos]
    )
    first_index = np.arange(PA)
    theta_one = angle_table(freq_one[:, :, None], first_index[None, None, :], PA)
    stage_one = constant(np.stack([np.cos(theta_one), -np.sin(theta_one)]))
    grid = jnp.einsum("pbrsn,pbsa->ran", turned, stage_one, precision=precise)
    return grid * (2.0 / L) ** 0.5


LANE = 128
SHIFTS = 8
CHUNK = 64


def stokes_body(k_ref, w_ref, o_ref, sh_ref):
    span = sh_ref.shape[1]
    total = w_ref.shape[1]
    steps = total // SHIFTS
    for s in range(SHIFTS):
        sh_ref[s] = k_ref[pl.ds(s, span), :]
    for part in range(total // CHUNK):

        def step(a, carry):
            acc_re, acc_im = carry
            base = pl.multiple_of(a * SHIFTS, SHIFTS)
            w_re = w_ref[0, pl.ds(base, SHIFTS), :]
            w_im = w_ref[1, pl.ds(base, SHIFTS), :]
            start = pl.multiple_of(part * CHUNK + total - SHIFTS - base, SHIFTS)
            for r in range(SHIFTS):
                slab = sh_ref[SHIFTS - 1 - r, pl.ds(start, CHUNK), :]
                acc_re = acc_re + slab * w_re[r : r + 1, :]
                acc_im = acc_im + slab * w_im[r : r + 1, :]
            return acc_re, acc_im

        zero = jnp.zeros((CHUNK, LANE), jnp.float32)
        acc_re, acc_im = lax.fori_loop(0, steps, step, (zero, zero), unroll=2)
        o_ref[0, part * CHUNK : (part + 1) * CHUNK, :] = acc_re
        o_ref[1, part * CHUNK : (part + 1) * CHUNK, :] = acc_im


def toeplitz_stokes(kernel_cols, weighted):
    taps, width = kernel_cols.shape
    total = weighted.shape[0]
    span = 2 * total
    flipped = jnp.pad(
        kernel_cols[::-1].astype(jnp.float32), ((0, span + SHIFTS - taps), (0, LANE - width))
    )
    source = jnp.pad(weighted.astype(jnp.float32).transpose(1, 0, 2), ((0, 0), (0, 0), (0, LANE - width)))
    out = pl.pallas_call(
        stokes_body,
        out_shape=jax.ShapeDtypeStruct((2, total, LANE), jnp.float32),
        scratch_shapes=[pltpu.VMEM((SHIFTS, span, LANE), jnp.float32)],
    )(flipped, source)
    return out[:, :, :width]


def per_device(gravity, coef, legendre, order_table, band_rows, kernel):
    bands = lax.axis_size("freq")
    blocks = lax.axis_size("lat")
    band_self = lax.axis_index("freq")
    block_self = lax.axis_index("lat")
    everyone = ("lat", "freq")
    devices = bands * blocks
    rows = gravity.shape[0]
    total_rows = rows * blocks
    mine = rows // bands
    band_width = kernel.shape[1]
    per_slot = coef.shape[0]
    held = blocks * per_slot
    sub = -(-band_width // blocks)
    share = sub - per_slot
    padded = held + share * blocks
    positions = order_table.reshape(blocks, bands, per_slot).transpose(1, 0, 2).reshape(bands, held) // bands
    selector = (
        positions[:, None, :] == jnp.arange(held, dtype=jnp.int32)[None, :, None]
    ).astype(jnp.float32)

    whole_rows = lax.all_to_all(gravity, "freq", split_axis=0, concat_axis=1, tiled=True)
    terms = forward_bands(whole_rows.reshape(mine, PA, PB), bands)
    own = jnp.einsum("brct,bts->brcs", terms[..., :held], selector, precision=precise)
    own = own.reshape(bands, mine, 2, blocks, per_slot)
    rest = jnp.pad(terms[..., held:], ((0, 0), (0, 0), (0, 0), (0, padded - band_width)))
    rest = rest.reshape(bands, mine, 2, blocks, share)
    my_rows = lax.dynamic_slice_in_dim(band_rows, band_self * mine, mine, 0)
    weight = jnp.cos((20.0 + my_rows.astype(jnp.float32) / 60.0) * (np.pi / 180.0))
    carried = jnp.broadcast_to(weight[None, :, None, None, None], (bands, mine, 2, blocks, 1))
    payload = jnp.concatenate([own, rest, carried], axis=4).transpose(3, 0, 1, 2, 4)
    payload = payload.reshape(devices, mine, 2, sub + 1)
    payload, coef, legendre = lax.optimization_barrier((payload, coef, legendre))
    observed = lax.all_to_all(payload, everyone, split_axis=0, concat_axis=0, tiled=True)
    observed = observed.reshape(total_rows, 2, sub + 1)
    weight_all = observed[:, 0, sub]
    observed = observed[:, :, :sub]

    synth = jnp.einsum("ocn,onq->ocq", coef, legendre, preferred_element_type=jnp.float32).astype(
        jnp.bfloat16
    )
    model = jnp.pad(synth.astype(jnp.float32).transpose(2, 1, 0), ((0, 0), (0, 0), (0, share)))
    weighted = ((observed - model) * weight_all[:, None, None]).astype(jnp.bfloat16)

    own_cols = lax.dynamic_slice_in_dim(positions[band_self], block_self * per_slot, per_slot, 0)
    kernel_own = jnp.take(kernel, own_cols, axis=1)
    kernel_rest = lax.dynamic_slice_in_dim(
        jnp.pad(kernel, ((0, 0), (0, padded - band_width))), held + block_self * share, share, 1
    )
    stokes = toeplitz_stokes(jnp.concatenate([kernel_own, kernel_rest], axis=1), weighted)
    stokes = stokes.reshape(2, devices, mine, sub).transpose(1, 2, 0, 3)
    by_source = lax.all_to_all(stokes, everyone, split_axis=0, concat_axis=0, tiled=True)
    by_source = by_source.reshape(blocks, bands, mine, 2, sub).transpose(1, 2, 3, 0, 4)
    slots_back = by_source[..., :per_slot].reshape(bands, mine, 2, held)
    slots_back = jnp.einsum("brcs,bts->brct", slots_back, selector, precision=precise)
    rest_back = by_source[..., per_slot:].reshape(bands, mine, 2, blocks * share)
    by_band = jnp.concatenate([slots_back, rest_back], axis=3)[..., :band_width]
    grid_rows = inverse_rows(by_band, bands)
    geoid = lax.all_to_all(grid_rows.reshape(mine, L), "freq", split_axis=1, concat_axis=0, tiled=True)
    return geoid


def solution(mesh):
    return jax.shard_map(
        per_device,
        mesh=mesh,
        in_specs=(
            P("lat", "freq"),
            P(("lat", "freq"), None, None),
            P(("lat", "freq"), None, None),
            P(),
            P("lat"),
            P(None, "freq"),
        ),
        out_specs=P("lat", "freq"),
        check_vma=False,
    )
```

```python
import jax
import jax.numpy as jnp
import numpy as np
from jax import lax
from jax.sharding import PartitionSpec as P
from jax.experimental import pallas as pl
from jax.experimental.pallas import tpu as pltpu

L = 21600
PA = 144
PB = 150
PH = 75


precise = lax.Precision.HIGH


def angle_table(first, second, period):
    phase = (first * second) % period
    return phase.astype(np.float64) * (2.0 * np.pi / period)


def constant(values):
    return jnp.asarray(np.asarray(values, dtype=np.float32))


def forward_bands(grid, bands):
    rows = grid.shape[0]
    first_index = np.arange(PA)
    theta_one = angle_table(first_index[:, None], first_index[None, :], PA)
    stage_one = constant(np.concatenate([np.cos(theta_one), -np.sin(theta_one)], axis=1))
    section = jnp.einsum("rab,ak->rbk", grid, stage_one, precision=precise)
    section_re = section[..., :PA]
    section_im = section[..., PA:]
    second_index = np.arange(PB)
    twist = angle_table(second_index[:, None], first_index[None, :], L)
    twist_cos = constant(np.cos(twist))
    twist_sin = constant(np.sin(twist))
    turned = jnp.concatenate(
        [section_re * twist_cos + section_im * twist_sin, section_im * twist_cos - section_re * twist_sin],
        axis=1,
    )
    freq_two = np.arange(PH)
    theta_two = angle_table(second_index[:, None], freq_two[None, :], PB)
    cos_two = np.cos(theta_two)
    sin_two = np.sin(theta_two)
    stage_two = constant(
        np.concatenate([np.concatenate([cos_two, -sin_two], axis=1), np.concatenate([sin_two, cos_two], axis=1)])
    )
    spec = jnp.einsum("rbk,bm->rkm", turned, stage_two, precision=precise)
    scale = (2.0 / L) ** 0.5
    stacked = spec.reshape(rows, PA, 2, PH).transpose(2, 0, 1, 3) * scale
    span = PA // bands
    stacked = stacked.reshape(2, rows, span, bands, PH).transpose(3, 1, 0, 4, 2)
    return stacked.reshape(bands, rows, 2, PH * span)


def inverse_rows(spectra, bands):
    rows = spectra.shape[1]
    span = PA // bands
    parts = spectra.reshape(bands, rows, 2 * PH, span)
    freq_two = np.arange(PH)
    second_index = np.arange(PB)
    theta_two = angle_table(freq_two[:, None], second_index[None, :], PB)
    cos_two = np.cos(theta_two)
    sin_two = np.sin(theta_two)
    stage_two = constant(
        np.concatenate([np.concatenate([cos_two, sin_two], axis=1), np.concatenate([-sin_two, cos_two], axis=1)])
    )
    middle = jnp.einsum("brms,mn->brsn", parts, stage_two, precision=precise)
    middle_re = middle[..., :PB]
    middle_im = middle[..., PB:]
    band_ids = np.arange(bands)
    freq_one = np.arange(span)[None, :] * bands + band_ids[:, None]
    twist = angle_table(freq_one[:, :, None], second_index[None, None, :], L)
    twist_cos = constant(np.cos(twist))[:, None]
    twist_sin = constant(np.sin(twist))[:, None]
    turned = jnp.stack(
        [middle_re * twist_cos - middle_im * twist_sin, middle_re * twist_sin + middle_im * twist_cos]
    )
    first_index = np.arange(PA)
    theta_one = angle_table(freq_one[:, :, None], first_index[None, None, :], PA)
    stage_one = constant(np.stack([np.cos(theta_one), -np.sin(theta_one)]))
    grid = jnp.einsum("pbrsn,pbsa->ran", turned, stage_one, precision=precise)
    return grid * (2.0 / L) ** 0.5


LANE = 128
SHIFTS = 8
CHUNK = 64


def stokes_body(k_ref, w_ref, o_ref, sh_ref):
    span = sh_ref.shape[1]
    total = w_ref.shape[1]
    steps = total // SHIFTS
    for s in range(SHIFTS):
        sh_ref[s] = k_ref[pl.ds(s, span), :]
    for part in range(total // CHUNK):

        def step(a, carry):
            acc_re, acc_im = carry
            base = pl.multiple_of(a * SHIFTS, SHIFTS)
            w_re = w_ref[0, pl.ds(base, SHIFTS), :]
            w_im = w_ref[1, pl.ds(base, SHIFTS), :]
            start = pl.multiple_of(part * CHUNK + total - SHIFTS - base, SHIFTS)
            for r in range(SHIFTS):
                slab = sh_ref[SHIFTS - 1 - r, pl.ds(start, CHUNK), :]
                acc_re = acc_re + slab * w_re[r : r + 1, :]
                acc_im = acc_im + slab * w_im[r : r + 1, :]
            return acc_re, acc_im

        zero = jnp.zeros((CHUNK, LANE), jnp.float32)
        acc_re, acc_im = lax.fori_loop(0, steps, step, (zero, zero))
        o_ref[0, part * CHUNK : (part + 1) * CHUNK, :] = acc_re
        o_ref[1, part * CHUNK : (part + 1) * CHUNK, :] = acc_im


def toeplitz_stokes(kernel_cols, weighted):
    taps, width = kernel_cols.shape
    total = weighted.shape[0]
    span = 2 * total
    flipped = jnp.pad(
        kernel_cols[::-1].astype(jnp.float32), ((0, span + SHIFTS - taps), (0, LANE - width))
    )
    source = jnp.pad(weighted.astype(jnp.float32).transpose(1, 0, 2), ((0, 0), (0, 0), (0, LANE - width)))
    out = pl.pallas_call(
        stokes_body,
        out_shape=jax.ShapeDtypeStruct((2, total, LANE), jnp.float32),
        scratch_shapes=[pltpu.VMEM((SHIFTS, span, LANE), jnp.float32)],
    )(flipped, source)
    return out[:, :, :width]


def exchanged(chunks, own, count):
    arrived = [chunks[own]]
    for shift in range(1, count):
        piece = lax.dynamic_index_in_dim(chunks, (own + shift) % count, 0, keepdims=False)
        route = [(i, (i + shift) % count) for i in range(count)]
        arrived.append(lax.ppermute(piece, "freq", route))
    by_shift = jnp.stack([arrived[(-j) % count] for j in range(count)])
    return jnp.roll(by_shift, own, axis=0)


def per_device(gravity, coef, legendre, order_table, band_rows, kernel):
    bands = lax.axis_size("freq")
    blocks = lax.axis_size("lat")
    band_self = lax.axis_index("freq")
    block_self = lax.axis_index("lat")
    everyone = ("lat", "freq")
    devices = bands * blocks
    rows = gravity.shape[0]
    total_rows = rows * blocks
    mine = rows // bands
    band_width = kernel.shape[1]
    per_slot = coef.shape[0]
    held = blocks * per_slot
    sub = -(-band_width // blocks)
    share = sub - per_slot
    padded = held + share * blocks
    positions = order_table.reshape(blocks, bands, per_slot).transpose(1, 0, 2).reshape(bands, held) // bands
    selector = (
        positions[:, None, :] == jnp.arange(held, dtype=jnp.int32)[None, :, None]
    ).astype(jnp.float32)

    whole_rows = lax.all_to_all(gravity, "freq", split_axis=0, concat_axis=1, tiled=True)
    terms = forward_bands(whole_rows.reshape(mine, PA, PB), bands)
    own = jnp.einsum("brct,bts->brcs", terms[..., :held], selector, precision=precise)
    own = own.reshape(bands, mine, 2, blocks, per_slot)
    rest = jnp.pad(terms[..., held:], ((0, 0), (0, 0), (0, 0), (0, padded - band_width)))
    rest = rest.reshape(bands, mine, 2, blocks, share)
    my_rows = lax.dynamic_slice_in_dim(band_rows, band_self * mine, mine, 0)
    weight = jnp.cos((20.0 + my_rows.astype(jnp.float32) / 60.0) * (np.pi / 180.0))
    carried = jnp.broadcast_to(weight[None, :, None, None, None], (bands, mine, 2, blocks, 1))
    payload = jnp.concatenate([own, rest, carried], axis=4).transpose(3, 0, 1, 2, 4)
    payload = payload.reshape(devices, mine, 2, sub + 1)
    payload, coef, legendre = lax.optimization_barrier((payload, coef, legendre))
    observed = lax.all_to_all(payload, everyone, split_axis=0, concat_axis=0, tiled=True)
    observed = observed.reshape(total_rows, 2, sub + 1)
    weight_all = observed[:, 0, sub]
    observed = observed[:, :, :sub]

    synth = jnp.einsum("ocn,onq->ocq", coef, legendre, preferred_element_type=jnp.float32).astype(
        jnp.bfloat16
    )
    model = jnp.pad(synth.astype(jnp.float32).transpose(2, 1, 0), ((0, 0), (0, 0), (0, share)))
    weighted = ((observed - model) * weight_all[:, None, None]).astype(jnp.bfloat16)

    own_cols = lax.dynamic_slice_in_dim(positions[band_self], block_self * per_slot, per_slot, 0)
    kernel_own = jnp.take(kernel, own_cols, axis=1)
    kernel_rest = lax.dynamic_slice_in_dim(
        jnp.pad(kernel, ((0, 0), (0, padded - band_width))), held + block_self * share, share, 1
    )
    stokes = toeplitz_stokes(jnp.concatenate([kernel_own, kernel_rest], axis=1), weighted)
    stokes = stokes.reshape(2, devices, mine, sub).transpose(1, 2, 0, 3)
    by_source = lax.all_to_all(stokes, everyone, split_axis=0, concat_axis=0, tiled=True)
    by_source = by_source.reshape(blocks, bands, mine, 2, sub).transpose(1, 2, 3, 0, 4)
    slots_back = by_source[..., :per_slot].reshape(bands, mine, 2, held)
    slots_back = jnp.einsum("brcs,bts->brct", slots_back, selector, precision=precise)
    rest_back = by_source[..., per_slot:].reshape(bands, mine, 2, blocks * share)
    by_band = jnp.concatenate([slots_back, rest_back], axis=3)[..., :band_width]
    grid_rows = inverse_rows(by_band, bands)
    geoid = exchanged(grid_rows.reshape(mine, bands, L // bands).transpose(1, 0, 2), band_self, bands)
    geoid = geoid.reshape(rows, L // bands)
    return geoid


def solution(mesh):
    return jax.shard_map(
        per_device,
        mesh=mesh,
        in_specs=(
            P("lat", "freq"),
            P(("lat", "freq"), None, None),
            P(("lat", "freq"), None, None),
            P(),
            P("lat"),
            P(None, "freq"),
        ),
        out_specs=P("lat", "freq"),
        check_vma=False,
    )
```

```python
import jax
import jax.numpy as jnp
import numpy as np
from jax import lax
from jax.sharding import PartitionSpec as P
from jax.experimental import pallas as pl
from jax.experimental.pallas import tpu as pltpu

L = 21600
PA = 144
PB = 150
PH = 75


precise = lax.Precision.HIGH


def angle_table(first, second, period):
    phase = (first * second) % period
    return phase.astype(np.float64) * (2.0 * np.pi / period)


def constant(values):
    return jnp.asarray(np.asarray(values, dtype=np.float32))


def forward_bands(grid, bands):
    rows = grid.shape[0]
    first_index = np.arange(PA)
    theta_one = angle_table(first_index[:, None], first_index[None, :], PA)
    stage_one = constant(np.concatenate([np.cos(theta_one), -np.sin(theta_one)], axis=1))
    section = jnp.einsum("rab,ak->rbk", grid, stage_one, precision=precise)
    section_re = section[..., :PA]
    section_im = section[..., PA:]
    second_index = np.arange(PB)
    twist = angle_table(second_index[:, None], first_index[None, :], L)
    twist_cos = constant(np.cos(twist))
    twist_sin = constant(np.sin(twist))
    turned = jnp.concatenate(
        [section_re * twist_cos + section_im * twist_sin, section_im * twist_cos - section_re * twist_sin],
        axis=1,
    )
    freq_two = np.arange(PH)
    theta_two = angle_table(second_index[:, None], freq_two[None, :], PB)
    cos_two = np.cos(theta_two)
    sin_two = np.sin(theta_two)
    stage_two = constant(
        np.concatenate([np.concatenate([cos_two, -sin_two], axis=1), np.concatenate([sin_two, cos_two], axis=1)])
    )
    spec = jnp.einsum("rbk,bm->rkm", turned, stage_two, precision=precise)
    scale = (2.0 / L) ** 0.5
    stacked = spec.reshape(rows, PA, 2, PH).transpose(2, 0, 1, 3) * scale
    span = PA // bands
    stacked = stacked.reshape(2, rows, span, bands, PH).transpose(3, 1, 0, 4, 2)
    return stacked.reshape(bands, rows, 2, PH * span)


def inverse_rows(spectra, bands):
    rows = spectra.shape[1]
    span = PA // bands
    parts = spectra.reshape(bands, rows, 2 * PH, span)
    freq_two = np.arange(PH)
    second_index = np.arange(PB)
    theta_two = angle_table(freq_two[:, None], second_index[None, :], PB)
    cos_two = np.cos(theta_two)
    sin_two = np.sin(theta_two)
    stage_two = constant(
        np.concatenate([np.concatenate([cos_two, sin_two], axis=1), np.concatenate([-sin_two, cos_two], axis=1)])
    )
    middle = jnp.einsum("brms,mn->brsn", parts, stage_two, precision=precise)
    middle_re = middle[..., :PB]
    middle_im = middle[..., PB:]
    band_ids = np.arange(bands)
    freq_one = np.arange(span)[None, :] * bands + band_ids[:, None]
    twist = angle_table(freq_one[:, :, None], second_index[None, None, :], L)
    twist_cos = constant(np.cos(twist))[:, None]
    twist_sin = constant(np.sin(twist))[:, None]
    turned = jnp.stack(
        [middle_re * twist_cos - middle_im * twist_sin, middle_re * twist_sin + middle_im * twist_cos]
    )
    first_index = np.arange(PA)
    theta_one = angle_table(freq_one[:, :, None], first_index[None, None, :], PA)
    stage_one = constant(np.stack([np.cos(theta_one), -np.sin(theta_one)]))
    grid = jnp.einsum("pbrsn,pbsa->ran", turned, stage_one, precision=precise)
    return grid * (2.0 / L) ** 0.5


LANE = 128
SHIFTS = 8
CHUNK = 64


def stokes_body(sh_ref, w_ref, o_ref):
    total = w_ref.shape[1]
    steps = total // SHIFTS
    for part in range(total // CHUNK):

        def step(a, carry):
            acc_re, acc_im = carry
            base = pl.multiple_of(a * SHIFTS, SHIFTS)
            w_re = w_ref[0, pl.ds(base, SHIFTS), :]
            w_im = w_ref[1, pl.ds(base, SHIFTS), :]
            start = pl.multiple_of(part * CHUNK + total - SHIFTS - base, SHIFTS)
            for r in range(SHIFTS):
                slab = sh_ref[SHIFTS - 1 - r, pl.ds(start, CHUNK), :]
                acc_re = acc_re + slab * w_re[r : r + 1, :]
                acc_im = acc_im + slab * w_im[r : r + 1, :]
            return acc_re, acc_im

        zero = jnp.zeros((CHUNK, LANE), jnp.float32)
        acc_re, acc_im = lax.fori_loop(0, steps, step, (zero, zero))
        o_ref[0, part * CHUNK : (part + 1) * CHUNK, :] = acc_re
        o_ref[1, part * CHUNK : (part + 1) * CHUNK, :] = acc_im


def toeplitz_stokes(kernel_cols, weighted):
    taps, width = kernel_cols.shape
    total = weighted.shape[0]
    span = 2 * total
    flipped = jnp.pad(
        kernel_cols[::-1].astype(jnp.float32), ((0, span + SHIFTS - taps), (0, LANE - width))
    )
    source = jnp.pad(weighted.astype(jnp.float32).transpose(1, 0, 2), ((0, 0), (0, 0), (0, LANE - width)))
    shifted = jnp.stack([flipped[s : s + span] for s in range(SHIFTS)])
    resident = pl.BlockSpec(memory_space=pltpu.VMEM)
    out = pl.pallas_call(
        stokes_body,
        in_specs=[resident, resident],
        out_specs=resident,
        out_shape=jax.ShapeDtypeStruct((2, total, LANE), jnp.float32),
    )(shifted, source)
    return out[:, :, :width]


def per_device(gravity, coef, legendre, order_table, band_rows, kernel):
    bands = lax.axis_size("freq")
    blocks = lax.axis_size("lat")
    band_self = lax.axis_index("freq")
    block_self = lax.axis_index("lat")
    everyone = ("lat", "freq")
    devices = bands * blocks
    rows = gravity.shape[0]
    total_rows = rows * blocks
    mine = rows // bands
    band_width = kernel.shape[1]
    per_slot = coef.shape[0]
    held = blocks * per_slot
    sub = -(-band_width // blocks)
    share = sub - per_slot
    padded = held + share * blocks
    positions = order_table.reshape(blocks, bands, per_slot).transpose(1, 0, 2).reshape(bands, held) // bands
    selector = (
        positions[:, None, :] == jnp.arange(held, dtype=jnp.int32)[None, :, None]
    ).astype(jnp.float32)

    whole_rows = lax.all_to_all(gravity, "freq", split_axis=0, concat_axis=1, tiled=True)
    terms = forward_bands(whole_rows.reshape(mine, PA, PB), bands)
    own = jnp.einsum("brct,bts->brcs", terms[..., :held], selector, precision=precise)
    own = own.reshape(bands, mine, 2, blocks, per_slot)
    rest = jnp.pad(terms[..., held:], ((0, 0), (0, 0), (0, 0), (0, padded - band_width)))
    rest = rest.reshape(bands, mine, 2, blocks, share)
    my_rows = lax.dynamic_slice_in_dim(band_rows, band_self * mine, mine, 0)
    weight = jnp.cos((20.0 + my_rows.astype(jnp.float32) / 60.0) * (np.pi / 180.0))
    carried = jnp.broadcast_to(weight[None, :, None, None, None], (bands, mine, 2, blocks, 1))
    payload = jnp.concatenate([own, rest, carried], axis=4).transpose(3, 0, 1, 2, 4)
    payload = payload.reshape(devices, mine, 2, sub + 1)
    payload, coef, legendre = lax.optimization_barrier((payload, coef, legendre))
    observed = lax.all_to_all(payload, everyone, split_axis=0, concat_axis=0, tiled=True)
    observed = observed.reshape(total_rows, 2, sub + 1)
    weight_all = observed[:, 0, sub]
    observed = observed[:, :, :sub]

    synth = jnp.einsum("ocn,onq->ocq", coef, legendre, preferred_element_type=jnp.float32).astype(
        jnp.bfloat16
    )
    model = jnp.pad(synth.astype(jnp.float32).transpose(2, 1, 0), ((0, 0), (0, 0), (0, share)))
    weighted = ((observed - model) * weight_all[:, None, None]).astype(jnp.bfloat16)

    own_cols = lax.dynamic_slice_in_dim(positions[band_self], block_self * per_slot, per_slot, 0)
    kernel_own = jnp.take(kernel, own_cols, axis=1)
    kernel_rest = lax.dynamic_slice_in_dim(
        jnp.pad(kernel, ((0, 0), (0, padded - band_width))), held + block_self * share, share, 1
    )
    stokes = toeplitz_stokes(jnp.concatenate([kernel_own, kernel_rest], axis=1), weighted)
    stokes = stokes.reshape(2, devices, mine, sub).transpose(1, 2, 0, 3)
    by_source = lax.all_to_all(stokes, everyone, split_axis=0, concat_axis=0, tiled=True)
    by_source = by_source.reshape(blocks, bands, mine, 2, sub).transpose(1, 2, 3, 0, 4)
    slots_back = by_source[..., :per_slot].reshape(bands, mine, 2, held)
    slots_back = jnp.einsum("brcs,bts->brct", slots_back, selector, precision=precise)
    rest_back = by_source[..., per_slot:].reshape(bands, mine, 2, blocks * share)
    by_band = jnp.concatenate([slots_back, rest_back], axis=3)[..., :band_width]
    grid_rows = inverse_rows(by_band, bands)
    geoid = lax.all_to_all(grid_rows.reshape(mine, L), "freq", split_axis=1, concat_axis=0, tiled=True)
    return geoid


def solution(mesh):
    return jax.shard_map(
        per_device,
        mesh=mesh,
        in_specs=(
            P("lat", "freq"),
            P(("lat", "freq"), None, None),
            P(("lat", "freq"), None, None),
            P(),
            P("lat"),
            P(None, "freq"),
        ),
        out_specs=P("lat", "freq"),
        check_vma=False,
    )
```

```python
import jax
import jax.numpy as jnp
import numpy as np
from jax import lax
from jax.sharding import PartitionSpec as P
from jax.experimental import pallas as pl
from jax.experimental.pallas import tpu as pltpu

L = 21600
PA = 144
PB = 150
PH = 75


precise = lax.Precision.HIGH


def angle_table(first, second, period):
    phase = (first * second) % period
    return phase.astype(np.float64) * (2.0 * np.pi / period)


def constant(values):
    return jnp.asarray(np.asarray(values, dtype=np.float32))


def forward_bands(grid, bands):
    rows = grid.shape[0]
    first_index = np.arange(PA)
    theta_one = angle_table(first_index[:, None], first_index[None, :], PA)
    stage_one = constant(np.concatenate([np.cos(theta_one), -np.sin(theta_one)], axis=1))
    section = jnp.einsum("rab,ak->rbk", grid, stage_one, precision=precise)
    section_re = section[..., :PA]
    section_im = section[..., PA:]
    second_index = np.arange(PB)
    twist = angle_table(second_index[:, None], first_index[None, :], L)
    twist_cos = constant(np.cos(twist))
    twist_sin = constant(np.sin(twist))
    turned = jnp.concatenate(
        [section_re * twist_cos + section_im * twist_sin, section_im * twist_cos - section_re * twist_sin],
        axis=1,
    )
    freq_two = np.arange(PH)
    theta_two = angle_table(second_index[:, None], freq_two[None, :], PB)
    cos_two = np.cos(theta_two)
    sin_two = np.sin(theta_two)
    stage_two = constant(
        np.concatenate([np.concatenate([cos_two, -sin_two], axis=1), np.concatenate([sin_two, cos_two], axis=1)])
    )
    spec = jnp.einsum("rbk,bm->rkm", turned, stage_two, precision=precise)
    scale = (2.0 / L) ** 0.5
    stacked = spec.reshape(rows, PA, 2, PH).transpose(2, 0, 1, 3) * scale
    span = PA // bands
    stacked = stacked.reshape(2, rows, span, bands, PH).transpose(3, 1, 0, 4, 2)
    return stacked.reshape(bands, rows, 2, PH * span)


def inverse_rows(spectra, bands):
    rows = spectra.shape[1]
    span = PA // bands
    parts = spectra.reshape(bands, rows, 2 * PH, span)
    freq_two = np.arange(PH)
    second_index = np.arange(PB)
    theta_two = angle_table(freq_two[:, None], second_index[None, :], PB)
    cos_two = np.cos(theta_two)
    sin_two = np.sin(theta_two)
    stage_two = constant(
        np.concatenate([np.concatenate([cos_two, sin_two], axis=1), np.concatenate([-sin_two, cos_two], axis=1)])
    )
    middle = jnp.einsum("brms,mn->brsn", parts, stage_two, precision=precise)
    middle_re = middle[..., :PB]
    middle_im = middle[..., PB:]
    band_ids = np.arange(bands)
    freq_one = np.arange(span)[None, :] * bands + band_ids[:, None]
    twist = angle_table(freq_one[:, :, None], second_index[None, None, :], L)
    twist_cos = constant(np.cos(twist))[:, None]
    twist_sin = constant(np.sin(twist))[:, None]
    turned = jnp.stack(
        [middle_re * twist_cos - middle_im * twist_sin, middle_re * twist_sin + middle_im * twist_cos]
    )
    first_index = np.arange(PA)
    theta_one = angle_table(freq_one[:, :, None], first_index[None, None, :], PA)
    stage_one = constant(np.stack([np.cos(theta_one), -np.sin(theta_one)]))
    grid = jnp.einsum("pbrsn,pbsa->ran", turned, stage_one, precision=precise)
    return grid * (2.0 / L) ** 0.5


LANE = 128
SHIFTS = 8
CHUNK = 128


def stokes_body(k_ref, w_ref, o_ref, sh_ref):
    span = sh_ref.shape[1]
    total = w_ref.shape[1]
    steps = total // SHIFTS
    for s in range(SHIFTS):
        sh_ref[s] = k_ref[pl.ds(s, span), :]
    for part in range(total // CHUNK):

        def step(a, carry):
            acc_re, acc_im = carry
            base = pl.multiple_of(a * SHIFTS, SHIFTS)
            w_re = w_ref[0, pl.ds(base, SHIFTS), :]
            w_im = w_ref[1, pl.ds(base, SHIFTS), :]
            start = pl.multiple_of(part * CHUNK + total - SHIFTS - base, SHIFTS)
            for r in range(SHIFTS):
                slab = sh_ref[SHIFTS - 1 - r, pl.ds(start, CHUNK), :]
                acc_re = acc_re + slab * w_re[r : r + 1, :]
                acc_im = acc_im + slab * w_im[r : r + 1, :]
            return acc_re, acc_im

        zero = jnp.zeros((CHUNK, LANE), jnp.float32)
        acc_re, acc_im = lax.fori_loop(0, steps, step, (zero, zero))
        o_ref[0, part * CHUNK : (part + 1) * CHUNK, :] = acc_re
        o_ref[1, part * CHUNK : (part + 1) * CHUNK, :] = acc_im


def toeplitz_stokes(kernel_cols, weighted):
    taps, width = kernel_cols.shape
    total = weighted.shape[0]
    span = 2 * total
    flipped = jnp.pad(
        kernel_cols[::-1].astype(jnp.float32), ((0, span + SHIFTS - taps), (0, LANE - width))
    )
    source = jnp.pad(weighted.astype(jnp.float32).transpose(1, 0, 2), ((0, 0), (0, 0), (0, LANE - width)))
    out = pl.pallas_call(
        stokes_body,
        out_shape=jax.ShapeDtypeStruct((2, total, LANE), jnp.float32),
        scratch_shapes=[pltpu.VMEM((SHIFTS, span, LANE), jnp.float32)],
    )(flipped, source)
    return out[:, :, :width]


def per_device(gravity, coef, legendre, order_table, band_rows, kernel):
    bands = lax.axis_size("freq")
    blocks = lax.axis_size("lat")
    band_self = lax.axis_index("freq")
    block_self = lax.axis_index("lat")
    everyone = ("lat", "freq")
    devices = bands * blocks
    rows = gravity.shape[0]
    total_rows = rows * blocks
    mine = rows // bands
    band_width = kernel.shape[1]
    per_slot = coef.shape[0]
    held = blocks * per_slot
    sub = -(-band_width // blocks)
    share = sub - per_slot
    padded = held + share * blocks
    positions = order_table.reshape(blocks, bands, per_slot).transpose(1, 0, 2).reshape(bands, held) // bands
    selector = (
        positions[:, None, :] == jnp.arange(held, dtype=jnp.int32)[None, :, None]
    ).astype(jnp.float32)

    whole_rows = lax.all_to_all(gravity, "freq", split_axis=0, concat_axis=1, tiled=True)
    terms = forward_bands(whole_rows.reshape(mine, PA, PB), bands)
    own = jnp.einsum("brct,bts->brcs", terms[..., :held], selector, precision=precise)
    own = own.reshape(bands, mine, 2, blocks, per_slot)
    rest = jnp.pad(terms[..., held:], ((0, 0), (0, 0), (0, 0), (0, padded - band_width)))
    rest = rest.reshape(bands, mine, 2, blocks, share)
    my_rows = lax.dynamic_slice_in_dim(band_rows, band_self * mine, mine, 0)
    weight = jnp.cos((20.0 + my_rows.astype(jnp.float32) / 60.0) * (np.pi / 180.0))
    carried = jnp.broadcast_to(weight[None, :, None, None, None], (bands, mine, 2, blocks, 1))
    payload = jnp.concatenate([own, rest, carried], axis=4).transpose(3, 0, 1, 2, 4)
    payload = payload.reshape(devices, mine, 2, sub + 1)
    payload, coef, legendre = lax.optimization_barrier((payload, coef, legendre))
    observed = lax.all_to_all(payload, everyone, split_axis=0, concat_axis=0, tiled=True)
    observed = observed.reshape(total_rows, 2, sub + 1)
    weight_all = observed[:, 0, sub]
    observed = observed[:, :, :sub]

    synth = jnp.einsum("ocn,onq->ocq", coef, legendre, preferred_element_type=jnp.float32).astype(
        jnp.bfloat16
    )
    model = jnp.pad(synth.astype(jnp.float32).transpose(2, 1, 0), ((0, 0), (0, 0), (0, share)))
    weighted = ((observed - model) * weight_all[:, None, None]).astype(jnp.bfloat16)

    own_cols = lax.dynamic_slice_in_dim(positions[band_self], block_self * per_slot, per_slot, 0)
    kernel_own = jnp.take(kernel, own_cols, axis=1)
    kernel_rest = lax.dynamic_slice_in_dim(
        jnp.pad(kernel, ((0, 0), (0, padded - band_width))), held + block_self * share, share, 1
    )
    stokes = toeplitz_stokes(jnp.concatenate([kernel_own, kernel_rest], axis=1), weighted)
    stokes = stokes.reshape(2, devices, mine, sub).transpose(1, 2, 0, 3)
    by_source = lax.all_to_all(stokes, everyone, split_axis=0, concat_axis=0, tiled=True)
    by_source = by_source.reshape(blocks, bands, mine, 2, sub).transpose(1, 2, 3, 0, 4)
    slots_back = by_source[..., :per_slot].reshape(bands, mine, 2, held)
    slots_back = jnp.einsum("brcs,bts->brct", slots_back, selector, precision=precise)
    rest_back = by_source[..., per_slot:].reshape(bands, mine, 2, blocks * share)
    by_band = jnp.concatenate([slots_back, rest_back], axis=3)[..., :band_width]
    grid_rows = inverse_rows(by_band, bands)
    geoid = lax.all_to_all(grid_rows.reshape(mine, L), "freq", split_axis=1, concat_axis=0, tiled=True)
    return geoid


def solution(mesh):
    return jax.shard_map(
        per_device,
        mesh=mesh,
        in_specs=(
            P("lat", "freq"),
            P(("lat", "freq"), None, None),
            P(("lat", "freq"), None, None),
            P(),
            P("lat"),
            P(None, "freq"),
        ),
        out_specs=P("lat", "freq"),
        check_vma=False,
    )
```

```python
import jax
import jax.numpy as jnp
import numpy as np
from jax import lax
from jax.sharding import PartitionSpec as P
from jax.experimental import pallas as pl
from jax.experimental.pallas import tpu as pltpu

L = 21600
PA = 144
PB = 150
PH = 75


precise = lax.Precision.HIGH


def angle_table(first, second, period):
    phase = (first * second) % period
    return phase.astype(np.float64) * (2.0 * np.pi / period)


def constant(values):
    return jnp.asarray(np.asarray(values, dtype=np.float32))


def forward_bands(grid, bands):
    rows = grid.shape[0]
    first_index = np.arange(PA)
    theta_one = angle_table(first_index[:, None], first_index[None, :], PA)
    stage_one = constant(np.concatenate([np.cos(theta_one), -np.sin(theta_one)], axis=1))
    section = jnp.einsum("rab,ak->rbk", grid, stage_one, precision=precise)
    section_re = section[..., :PA]
    section_im = section[..., PA:]
    second_index = np.arange(PB)
    twist = angle_table(second_index[:, None], first_index[None, :], L)
    twist_cos = constant(np.cos(twist))
    twist_sin = constant(np.sin(twist))
    turned = jnp.concatenate(
        [section_re * twist_cos + section_im * twist_sin, section_im * twist_cos - section_re * twist_sin],
        axis=1,
    )
    freq_two = np.arange(PH)
    theta_two = angle_table(second_index[:, None], freq_two[None, :], PB)
    cos_two = np.cos(theta_two)
    sin_two = np.sin(theta_two)
    stage_two = constant(
        np.concatenate([np.concatenate([cos_two, -sin_two], axis=1), np.concatenate([sin_two, cos_two], axis=1)])
    )
    spec = jnp.einsum("rbk,bm->rkm", turned, stage_two, precision=precise)
    scale = (2.0 / L) ** 0.5
    stacked = spec.reshape(rows, PA, 2, PH).transpose(2, 0, 1, 3) * scale
    span = PA // bands
    stacked = stacked.reshape(2, rows, span, bands, PH).transpose(3, 1, 0, 4, 2)
    return stacked.reshape(bands, rows, 2, PH * span)


def inverse_rows(spectra, bands):
    rows = spectra.shape[1]
    span = PA // bands
    parts = spectra.reshape(bands, rows, 2 * PH, span)
    freq_two = np.arange(PH)
    second_index = np.arange(PB)
    theta_two = angle_table(freq_two[:, None], second_index[None, :], PB)
    cos_two = np.cos(theta_two)
    sin_two = np.sin(theta_two)
    stage_two = constant(
        np.concatenate([np.concatenate([cos_two, sin_two], axis=1), np.concatenate([-sin_two, cos_two], axis=1)])
    )
    middle = jnp.einsum("brms,mn->brsn", parts, stage_two, precision=precise)
    middle_re = middle[..., :PB]
    middle_im = middle[..., PB:]
    band_ids = np.arange(bands)
    freq_one = np.arange(span)[None, :] * bands + band_ids[:, None]
    twist = angle_table(freq_one[:, :, None], second_index[None, None, :], L)
    twist_cos = constant(np.cos(twist))[:, None]
    twist_sin = constant(np.sin(twist))[:, None]
    turned = jnp.stack(
        [middle_re * twist_cos - middle_im * twist_sin, middle_re * twist_sin + middle_im * twist_cos]
    )
    first_index = np.arange(PA)
    theta_one = angle_table(freq_one[:, :, None], first_index[None, None, :], PA)
    stage_one = constant(np.stack([np.cos(theta_one), -np.sin(theta_one)]))
    grid = jnp.einsum("pbrsn,pbsa->ran", turned, stage_one, precision=precise)
    return grid * (2.0 / L) ** 0.5


LANE = 128
SHIFTS = 8
CHUNK = 32


def stokes_body(k_ref, w_ref, o_ref, sh_ref):
    span = sh_ref.shape[1]
    total = w_ref.shape[1]
    steps = total // SHIFTS
    for s in range(SHIFTS):
        sh_ref[s] = k_ref[pl.ds(s, span), :]
    for part in range(total // CHUNK):

        def step(a, carry):
            acc_re, acc_im = carry
            base = pl.multiple_of(a * SHIFTS, SHIFTS)
            w_re = w_ref[0, pl.ds(base, SHIFTS), :]
            w_im = w_ref[1, pl.ds(base, SHIFTS), :]
            start = pl.multiple_of(part * CHUNK + total - SHIFTS - base, SHIFTS)
            for r in range(SHIFTS):
                slab = sh_ref[SHIFTS - 1 - r, pl.ds(start, CHUNK), :]
                acc_re = acc_re + slab * w_re[r : r + 1, :]
                acc_im = acc_im + slab * w_im[r : r + 1, :]
            return acc_re, acc_im

        zero = jnp.zeros((CHUNK, LANE), jnp.float32)
        acc_re, acc_im = lax.fori_loop(0, steps, step, (zero, zero))
        o_ref[0, part * CHUNK : (part + 1) * CHUNK, :] = acc_re
        o_ref[1, part * CHUNK : (part + 1) * CHUNK, :] = acc_im


def toeplitz_stokes(kernel_cols, weighted):
    taps, width = kernel_cols.shape
    total = weighted.shape[0]
    span = 2 * total
    flipped = jnp.pad(
        kernel_cols[::-1].astype(jnp.float32), ((0, span + SHIFTS - taps), (0, LANE - width))
    )
    source = jnp.pad(weighted.astype(jnp.float32).transpose(1, 0, 2), ((0, 0), (0, 0), (0, LANE - width)))
    out = pl.pallas_call(
        stokes_body,
        out_shape=jax.ShapeDtypeStruct((2, total, LANE), jnp.float32),
        scratch_shapes=[pltpu.VMEM((SHIFTS, span, LANE), jnp.float32)],
    )(flipped, source)
    return out[:, :, :width]


def per_device(gravity, coef, legendre, order_table, band_rows, kernel):
    bands = lax.axis_size("freq")
    blocks = lax.axis_size("lat")
    band_self = lax.axis_index("freq")
    block_self = lax.axis_index("lat")
    everyone = ("lat", "freq")
    devices = bands * blocks
    rows = gravity.shape[0]
    total_rows = rows * blocks
    mine = rows // bands
    band_width = kernel.shape[1]
    per_slot = coef.shape[0]
    held = blocks * per_slot
    sub = -(-band_width // blocks)
    share = sub - per_slot
    padded = held + share * blocks
    positions = order_table.reshape(blocks, bands, per_slot).transpose(1, 0, 2).reshape(bands, held) // bands
    selector = (
        positions[:, None, :] == jnp.arange(held, dtype=jnp.int32)[None, :, None]
    ).astype(jnp.float32)

    whole_rows = lax.all_to_all(gravity, "freq", split_axis=0, concat_axis=1, tiled=True)
    terms = forward_bands(whole_rows.reshape(mine, PA, PB), bands)
    own = jnp.einsum("brct,bts->brcs", terms[..., :held], selector, precision=precise)
    own = own.reshape(bands, mine, 2, blocks, per_slot)
    rest = jnp.pad(terms[..., held:], ((0, 0), (0, 0), (0, 0), (0, padded - band_width)))
    rest = rest.reshape(bands, mine, 2, blocks, share)
    my_rows = lax.dynamic_slice_in_dim(band_rows, band_self * mine, mine, 0)
    weight = jnp.cos((20.0 + my_rows.astype(jnp.float32) / 60.0) * (np.pi / 180.0))
    carried = jnp.broadcast_to(weight[None, :, None, None, None], (bands, mine, 2, blocks, 1))
    payload = jnp.concatenate([own, rest, carried], axis=4).transpose(3, 0, 1, 2, 4)
    payload = payload.reshape(devices, mine, 2, sub + 1)
    payload, coef, legendre = lax.optimization_barrier((payload, coef, legendre))
    observed = lax.all_to_all(payload, everyone, split_axis=0, concat_axis=0, tiled=True)
    observed = observed.reshape(total_rows, 2, sub + 1)
    weight_all = observed[:, 0, sub]
    observed = observed[:, :, :sub]

    synth = jnp.einsum("ocn,onq->ocq", coef, legendre, preferred_element_type=jnp.float32).astype(
        jnp.bfloat16
    )
    model = jnp.pad(synth.astype(jnp.float32).transpose(2, 1, 0), ((0, 0), (0, 0), (0, share)))
    weighted = ((observed - model) * weight_all[:, None, None]).astype(jnp.bfloat16)

    own_cols = lax.dynamic_slice_in_dim(positions[band_self], block_self * per_slot, per_slot, 0)
    kernel_own = jnp.take(kernel, own_cols, axis=1)
    kernel_rest = lax.dynamic_slice_in_dim(
        jnp.pad(kernel, ((0, 0), (0, padded - band_width))), held + block_self * share, share, 1
    )
    stokes = toeplitz_stokes(jnp.concatenate([kernel_own, kernel_rest], axis=1), weighted)
    stokes = stokes.reshape(2, devices, mine, sub).transpose(1, 2, 0, 3)
    by_source = lax.all_to_all(stokes, everyone, split_axis=0, concat_axis=0, tiled=True)
    by_source = by_source.reshape(blocks, bands, mine, 2, sub).transpose(1, 2, 3, 0, 4)
    slots_back = by_source[..., :per_slot].reshape(bands, mine, 2, held)
    slots_back = jnp.einsum("brcs,bts->brct", slots_back, selector, precision=precise)
    rest_back = by_source[..., per_slot:].reshape(bands, mine, 2, blocks * share)
    by_band = jnp.concatenate([slots_back, rest_back], axis=3)[..., :band_width]
    grid_rows = inverse_rows(by_band, bands)
    geoid = lax.all_to_all(grid_rows.reshape(mine, L), "freq", split_axis=1, concat_axis=0, tiled=True)
    return geoid


def solution(mesh):
    return jax.shard_map(
        per_device,
        mesh=mesh,
        in_specs=(
            P("lat", "freq"),
            P(("lat", "freq"), None, None),
            P(("lat", "freq"), None, None),
            P(),
            P("lat"),
            P(None, "freq"),
        ),
        out_specs=P("lat", "freq"),
        check_vma=False,
    )
```
